256 devices in a mesh: wide: 16 (over z, core), narrow: 16 (over y, x).
Axes of the slice: x: 4, y: 4, z: 8, core: 2. Of those that a mesh axis runs over, the one named last changes fastest.
Arguments:
- screens: bfloat16 [4, 4096, 4096], P(None, 'wide'), may hold values from -3 to 3
- offsets: int32 [2, 128, 4], replicated, may hold values from 0 to 2752, as said below
- valid: int32 [2, 80, 80], P(None, 'narrow'), may hold values from 0 to 1, as said below
- recon: bfloat16 [25600, 5120], P('narrow', 'wide'), may hold values from -0.0390625 to 0.0390625
Outputs:
- slopes: float32 [2, 64, 2, 80, 80], P(None, 'wide', None, 'narrow')
- commands: float32 [64, 5120], P('narrow', 'wide')
The draws below stay inside these ranges and needn't reach their ends.
Inputs may be any that keep to these rules, and one draw needn't show every extreme that they name: For each coordinate and each layer, the offsets of all items lie within 64 of the smallest, and the largest is exactly 64 above the smallest. In the 5 subaperture rows of one index of narrow, each sensor has at most 300 valid subapertures; in every draw one index of narrow holds exactly 300 for each sensor.
All inputs are finite; a program needn't handle non-finite values.
Results may differ from the reference program's by a relative error of at most 0.0043.
Values may be sent and summed in bfloat16 or wider, within the bound.
No kernel may reach another device: no remote copies, remote signals or barrier semaphores. Data moves between devices by JAX's collectives and lax.ppermute only.
A program may use at most 128 MiB of HBM per device.

```python
import math
import jax
import jax.numpy as jnp
from jax import lax

G = 4096
L = 4
NSUB = 80
SAMP = 16
NPIX = 32
NSENS = 2
SPREAD = 64
ACT = 5120
FRAMES = 64
ITEMS = 128
PUP = 1280
SROWS = 5
CAPS = 300
NSL = 25600


def draw_offsets(key, part):
    key_base, key_spread, key_pick = jax.random.split(key, 3)
    top_value = G - PUP - 2 * SPREAD
    base_offset = jax.random.randint(key_base, (2, 1, L), 0, top_value + 1)
    layer_ids = jnp.arange(L, dtype=jnp.int32)[None, None, :]
    coord_ids = jnp.arange(2, dtype=jnp.int32)[:, None, None]
    base_offset = jnp.where((layer_ids == 0) & (coord_ids == 0), top_value, base_offset)
    base_offset = jnp.where((layer_ids == 0) & (coord_ids == 1), 0, base_offset)
    spread = jax.random.randint(key_spread, (2, ITEMS, L), 0, SPREAD + 1)
    scores = jax.random.randint(key_pick, (2, L, ITEMS), 0, 1 << 18) * ITEMS + jnp.arange(ITEMS, dtype=jnp.int32)[None, None, :]
    sort_order = jnp.argsort(scores, axis=2)
    low_item = sort_order[:, :, 0]
    high_item = sort_order[:, :, 1]
    item_ids = jnp.arange(ITEMS, dtype=jnp.int32)[None, :, None]
    spread = jnp.where(item_ids == low_item[:, None, :], 0, spread)
    spread = jnp.where(item_ids == high_item[:, None, :], SPREAD, spread)
    return (base_offset + spread).astype(jnp.int32)


def draw_valid(key, part):
    key_count, key_peak, key_place = jax.random.split(key, 3)
    blocks = NSUB // SROWS
    cells = SROWS * NSUB
    counts = jax.random.randint(key_count, (NSENS, blocks), CAPS // 8, 3 * CAPS // 4 + 1)
    peak_block = jax.random.randint(key_peak, (), 0, blocks)
    counts = jnp.where(jnp.arange(blocks, dtype=jnp.int32)[None, :] == peak_block, CAPS, counts)
    scores = jax.random.randint(key_place, (NSENS, blocks, cells), 0, 1 << 18) * cells + jnp.arange(cells, dtype=jnp.int32)[None, None, :]
    ranks = jnp.argsort(jnp.argsort(scores, axis=2), axis=2)
    valid_flags = (ranks < counts[:, :, None]).astype(jnp.int32)
    return valid_flags.reshape(NSENS, NSUB, NSUB)


def steps_of(own_key, dims, cuts, smallest, high):
    def one(dim, shards_of):
        heights = jax.random.uniform(jax.random.fold_in(jax.random.fold_in(own_key, 6), dim), (shards_of,), jnp.float32, smallest / len(cuts), high / len(cuts))
        return jnp.repeat(jnp.exp(heights), dims[dim] // shards_of).reshape((-1,) + (1,) * (len(dims) - dim - 1))

    factor_of = one(*cuts[0])
    for cut in cuts[1:]:
        factor_of = factor_of * one(*cut)
    return factor_of


def noise(stream_key, dims, scale, reach, cuts=(), held_as=jnp.bfloat16):
    values = jax.random.normal(stream_key, dims, jnp.float32) * scale
    if len(cuts) > 0:
        values = steps_of(stream_key, dims, cuts, -0.22, 0.18) * values
    return jnp.clip(values, min=-reach, max=reach).astype(held_as)


def setup_inputs(seed: int = 0) -> dict:
    splits = jax.random.split(jax.random.key(seed), 5)
    return {
        "screens": noise(splits[0], (L, G, G), 0.5, 3.0, ((1, 16),)),
        "offsets": draw_offsets(jax.random.fold_in(splits[4], 71), 0),
        "valid": draw_valid(jax.random.fold_in(splits[4], 71), 0),
        "recon": noise(splits[3], (NSL, ACT), NSL ** -0.5, 0.0390625, ((0, 16), (1, 16))),
    }


def dft_table(samp, npix):
    sample_ids = jnp.arange(samp * samp, dtype=jnp.int32)
    pixel_ids = jnp.arange(npix * npix, dtype=jnp.int32)
    sample_row = sample_ids // samp
    sample_col = sample_ids % samp
    pixel_row = pixel_ids // npix - npix // 2
    pixel_col = pixel_ids % npix - npix // 2
    phase_turns = jnp.mod(sample_row[:, None] * pixel_row[None, :] + sample_col[:, None] * pixel_col[None, :], npix)
    angles = phase_turns.astype(jnp.float32) * jnp.float32(-2.0 * math.pi / npix)
    cosine = jnp.cos(angles).astype(jnp.bfloat16)
    sine_part = jnp.sin(angles).astype(jnp.bfloat16)
    top_rows = jnp.concatenate([cosine, sine_part], axis=1)
    bottom_rows = jnp.concatenate([-sine_part, cosine], axis=1)
    return jnp.concatenate([top_rows, bottom_rows], axis=0)


def subaperture_fields(pupil_phase, samp):
    sub_rows = pupil_phase.shape[0] // samp
    sub_cols = pupil_phase.shape[1] // samp
    samples = pupil_phase.reshape(sub_rows, samp, sub_cols, samp).transpose(0, 2, 1, 3).reshape(sub_rows * sub_cols, samp * samp)
    return jnp.concatenate([jnp.cos(samples), jnp.sin(samples)], axis=1).astype(jnp.bfloat16)


def centroids(fields, transform, npix):
    spectrum = jnp.dot(fields, transform, preferred_element_type=jnp.float32)
    pixel_count = npix * npix
    real_part = spectrum[:, :pixel_count]
    imag_part = spectrum[:, pixel_count:]
    intensity = real_part * real_part + imag_part * imag_part
    pixel_ids = jnp.arange(pixel_count, dtype=jnp.int32)
    along_x = (pixel_ids % npix - npix // 2).astype(jnp.float32)
    along_y = (pixel_ids // npix - npix // 2).astype(jnp.float32)
    flux_total = jnp.sum(intensity, axis=1)
    centre_x = jnp.sum(intensity * along_x[None, :], axis=1) / flux_total
    centre_y = jnp.sum(intensity * along_y[None, :], axis=1) / flux_total
    return jnp.stack([centre_x, centre_y], axis=1)


def reference(screens, offsets, valid, recon):
    transform = dft_table(SAMP, NPIX)

    def one_item(item_index):
        pupil_phase = jnp.zeros((PUP, PUP), jnp.float32)
        for which_layer in range(L):
            window = lax.dynamic_slice(screens[which_layer], (offsets[0, item_index, which_layer], offsets[1, item_index, which_layer]), (PUP, PUP))
            pupil_phase = pupil_phase + window.astype(jnp.float32)
        return centroids(subaperture_fields(pupil_phase, SAMP), transform, NPIX)

    measured = lax.map(one_item, jnp.arange(ITEMS, dtype=jnp.int32))
    measured = measured.reshape(FRAMES, NSENS, NSUB, NSUB, 2) * valid[None, :, :, :, None].astype(jnp.float32)
    slopes = measured.transpose(4, 0, 1, 2, 3)
    slope_vector = measured.transpose(0, 2, 1, 3, 4).reshape(FRAMES, NSL).astype(jnp.bfloat16)
    commands = jnp.dot(slope_vector, recon, preferred_element_type=jnp.float32)
    return slopes, commands
```

```python
import math

import jax
import jax.numpy as jnp
from jax import lax
from jax.sharding import PartitionSpec as P

L = 4
NSUB = 80
SAMP = 16
NPIX = 32
NSENS = 2
SPREAD = 64
FR_DEV = 4
PUP = 1280


def broadcast(block, axis, source):
    block = jnp.where(lax.axis_index(axis) == source, block, jnp.zeros_like(block))
    return lax.psum(block, axis)


def dft_table(samp, npix):
    sample_ids = jnp.arange(samp * samp, dtype=jnp.int32)
    pixel_ids = jnp.arange(npix * npix, dtype=jnp.int32)
    sample_row = sample_ids // samp
    sample_col = sample_ids % samp
    pixel_row = pixel_ids // npix - npix // 2
    pixel_col = pixel_ids % npix - npix // 2
    phase_turns = jnp.mod(
        sample_row[:, None] * pixel_row[None, :] + sample_col[:, None] * pixel_col[None, :], npix
    )
    angles = phase_turns.astype(jnp.float32) * jnp.float32(-2.0 * math.pi / npix)
    cosine = jnp.cos(angles).astype(jnp.bfloat16)
    sine_part = jnp.sin(angles).astype(jnp.bfloat16)
    top_rows = jnp.concatenate([cosine, sine_part], axis=1)
    bottom_rows = jnp.concatenate([-sine_part, cosine], axis=1)
    return jnp.concatenate([top_rows, bottom_rows], axis=0)


def subaperture_fields(pupil_phase, samp):
    sub_rows = pupil_phase.shape[0] // samp
    sub_cols = pupil_phase.shape[1] // samp
    samples = (
        pupil_phase.reshape(sub_rows, samp, sub_cols, samp)
        .transpose(0, 2, 1, 3)
        .reshape(sub_rows * sub_cols, samp * samp)
    )
    return jnp.concatenate([jnp.cos(samples), jnp.sin(samples)], axis=1).astype(jnp.bfloat16)


def centroids(fields, transform, npix):
    spectrum = jnp.dot(fields, transform, preferred_element_type=jnp.float32)
    pixel_count = npix * npix
    real_part = spectrum[:, :pixel_count]
    imag_part = spectrum[:, pixel_count:]
    intensity = real_part * real_part + imag_part * imag_part
    pixel_ids = jnp.arange(pixel_count, dtype=jnp.int32)
    along_x = (pixel_ids % npix - npix // 2).astype(jnp.float32)
    along_y = (pixel_ids // npix - npix // 2).astype(jnp.float32)
    flux_total = jnp.sum(intensity, axis=1)
    centre_x = jnp.sum(intensity * along_x[None, :], axis=1) / flux_total
    centre_y = jnp.sum(intensity * along_y[None, :], axis=1) / flux_total
    return jnp.stack([centre_x, centre_y], axis=1)


def body(screens, offsets, valid, recon):
    wide_index = lax.axis_index("wide")
    narrow_index = lax.axis_index("narrow")
    band_rows = screens.shape[1]
    sub_rows = valid.shape[1]
    pixel_rows = sub_rows * SAMP
    slab_rows = pixel_rows + SPREAD
    union_cols = PUP + SPREAD
    local_items = FR_DEV * NSENS
    own_offsets = lax.dynamic_slice_in_dim(offsets, wide_index * local_items, local_items, 1)
    lowest = jnp.min(offsets, axis=1)
    pad = jnp.zeros((slab_rows, union_cols), screens.dtype)
    slabs = []
    for which_layer in range(L):
        band = lax.dynamic_slice_in_dim(screens[which_layer], lowest[1, which_layer], union_cols, 1)
        padded = jnp.concatenate([pad, band, pad], axis=0)
        group_start = lowest[0, which_layer] + pixel_rows * narrow_index
        row_at = jnp.clip(group_start - wide_index * band_rows + slab_rows, 0, band_rows + slab_rows)
        slabs.append(lax.dynamic_slice_in_dim(padded, row_at, slab_rows, 0))
    slabs = lax.psum(jnp.stack(slabs), "wide")
    rel = own_offsets - lowest[:, None, :]
    phases = []
    for item in range(local_items):
        acc = jnp.zeros((pixel_rows, PUP), jnp.float32)
        for which_layer in range(L):
            window = lax.dynamic_slice(
                slabs[which_layer], (rel[0, item, which_layer], rel[1, item, which_layer]), (pixel_rows, PUP)
            )
            acc = acc + window.astype(jnp.float32)
        phases.append(acc)
    pupil_phase = jnp.stack(phases)
    transform = dft_table(SAMP, NPIX)
    frame_phase = pupil_phase.reshape(FR_DEV, NSENS, pixel_rows, PUP)
    valid_flags = valid.reshape(-1)

    def frame_fields(frame_block):
        return jnp.concatenate(
            [subaperture_fields(frame_block[sensor_index], SAMP) for sensor_index in range(NSENS)],
            axis=0,
        )

    def one_frame(frame_block):
        return centroids(frame_fields(frame_block), transform, NPIX) * valid_flags[:, None].astype(
            jnp.float32
        )

    measured = lax.map(one_frame, frame_phase)
    measured = measured.reshape(FR_DEV, NSENS, sub_rows, NSUB, 2)
    slopes = measured.transpose(4, 0, 1, 2, 3)
    slope_vector = (
        measured.transpose(0, 2, 1, 3, 4)
        .reshape(FR_DEV, sub_rows * NSENS * NSUB * 2)
        .astype(jnp.bfloat16)
    )
    partial_commands = jnp.dot(
        lax.all_gather(slope_vector, "wide", axis=0, tiled=True),
        recon,
        preferred_element_type=jnp.float32,
    )
    commands = lax.psum_scatter(partial_commands, "narrow", scatter_dimension=0, tiled=True)
    return (slopes, commands)


def solution(mesh):
    return jax.shard_map(
        body,
        mesh=mesh,
        in_specs=(P(None, "wide", None), P(), P(None, "narrow", None), P("narrow", "wide")),
        out_specs=(P(None, "wide", None, "narrow", None), P("narrow", "wide")),
        check_vma=False,
    )
```

```python
import math

import jax
import jax.numpy as jnp
from jax import lax
from jax.sharding import PartitionSpec as P

L = 4
NSUB = 80
SAMP = 16
NPIX = 32
NSENS = 2
SPREAD = 64
FR_DEV = 4
PUP = 1280


def broadcast(block, axis, source):
    block = jnp.where(lax.axis_index(axis) == source, block, jnp.zeros_like(block))
    return lax.psum(block, axis)


def dft_table(samp, npix):
    sample_ids = jnp.arange(samp * samp, dtype=jnp.int32)
    pixel_ids = jnp.arange(npix * npix, dtype=jnp.int32)
    sample_row = sample_ids // samp
    sample_col = sample_ids % samp
    pixel_row = pixel_ids // npix - npix // 2
    pixel_col = pixel_ids % npix - npix // 2
    phase_turns = jnp.mod(
        sample_row[:, None] * pixel_row[None, :] + sample_col[:, None] * pixel_col[None, :], npix
    )
    angles = phase_turns.astype(jnp.float32) * jnp.float32(-2.0 * math.pi / npix)
    cosine = jnp.cos(angles).astype(jnp.bfloat16)
    sine_part = jnp.sin(angles).astype(jnp.bfloat16)
    top_rows = jnp.concatenate([cosine, sine_part], axis=1)
    bottom_rows = jnp.concatenate([-sine_part, cosine], axis=1)
    return jnp.concatenate([top_rows, bottom_rows], axis=0)


def subaperture_fields(pupil_phase, samp):
    sub_rows = pupil_phase.shape[0] // samp
    sub_cols = pupil_phase.shape[1] // samp
    samples = (
        pupil_phase.reshape(sub_rows, samp, sub_cols, samp)
        .transpose(0, 2, 1, 3)
        .reshape(sub_rows * sub_cols, samp * samp)
    )
    return jnp.concatenate([jnp.cos(samples), jnp.sin(samples)], axis=1).astype(jnp.bfloat16)


def centroids(fields, transform, npix):
    spectrum = jnp.dot(fields, transform, preferred_element_type=jnp.float32)
    pixel_count = npix * npix
    real_part = spectrum[:, :pixel_count]
    imag_part = spectrum[:, pixel_count:]
    intensity = real_part * real_part + imag_part * imag_part
    pixel_ids = jnp.arange(pixel_count, dtype=jnp.int32)
    along_x = (pixel_ids % npix - npix // 2).astype(jnp.float32)
    along_y = (pixel_ids // npix - npix // 2).astype(jnp.float32)
    flux_total = jnp.sum(intensity, axis=1)
    centre_x = jnp.sum(intensity * along_x[None, :], axis=1) / flux_total
    centre_y = jnp.sum(intensity * along_y[None, :], axis=1) / flux_total
    return jnp.stack([centre_x, centre_y], axis=1)


def body(screens, offsets, valid, recon):
    wide_count = lax.axis_size("wide")
    narrow_count = lax.axis_size("narrow")
    wide_index = lax.axis_index("wide")
    narrow_index = lax.axis_index("narrow")
    band_rows = screens.shape[1]
    sub_rows = valid.shape[1]
    pixel_rows = sub_rows * SAMP
    slab_rows = pixel_rows + SPREAD
    union_cols = PUP + SPREAD
    local_items = FR_DEV * NSENS
    own_offsets = lax.dynamic_slice_in_dim(offsets, wide_index * local_items, local_items, 1)
    lowest = jnp.min(offsets, axis=1)
    pad = jnp.zeros((slab_rows, union_cols), screens.dtype)
    slabs = []
    for which_layer in range(L):
        band = lax.dynamic_slice_in_dim(screens[which_layer], lowest[1, which_layer], union_cols, 1)
        padded = jnp.concatenate([pad, band, pad], axis=0)
        group_start = lowest[0, which_layer] + pixel_rows * narrow_index
        row_at = jnp.clip(group_start - wide_index * band_rows + slab_rows, 0, band_rows + slab_rows)
        slabs.append(lax.dynamic_slice_in_dim(padded, row_at, slab_rows, 0))
    slabs = jnp.stack(slabs).reshape(wide_count, L * slab_rows // wide_count, union_cols)
    slabs = jnp.sum(lax.all_to_all(slabs, "wide", 0, 0), axis=0, dtype=slabs.dtype)
    slabs = lax.all_gather(slabs, "wide", axis=0, tiled=True).reshape(L, slab_rows, union_cols)
    rel = own_offsets - lowest[:, None, :]
    phases = []
    for item in range(local_items):
        acc = jnp.zeros((pixel_rows, PUP), jnp.float32)
        for which_layer in range(L):
            window = lax.dynamic_slice(
                slabs[which_layer], (rel[0, item, which_layer], rel[1, item, which_layer]), (pixel_rows, PUP)
            )
            acc = acc + window.astype(jnp.float32)
        phases.append(acc)
    pupil_phase = jnp.stack(phases)
    transform = dft_table(SAMP, NPIX)
    frame_phase = pupil_phase.reshape(FR_DEV, NSENS, pixel_rows, PUP)
    valid_flags = valid.reshape(-1)

    def frame_fields(frame_block):
        return jnp.concatenate(
            [subaperture_fields(frame_block[sensor_index], SAMP) for sensor_index in range(NSENS)],
            axis=0,
        )

    def one_frame(frame_block):
        return centroids(frame_fields(frame_block), transform, NPIX) * valid_flags[:, None].astype(
            jnp.float32
        )

    measured = lax.map(one_frame, frame_phase)
    measured = measured.reshape(FR_DEV, NSENS, sub_rows, NSUB, 2)
    slopes = measured.transpose(4, 0, 1, 2, 3)
    slope_vector = (
        measured.transpose(0, 2, 1, 3, 4)
        .reshape(FR_DEV, sub_rows * NSENS * NSUB * 2)
        .astype(jnp.bfloat16)
    )
    partial_commands = jnp.dot(
        lax.all_gather(slope_vector, "wide", axis=0, tiled=True),
        recon,
        preferred_element_type=jnp.float32,
    )
    partial_commands = partial_commands.reshape(narrow_count, -1, partial_commands.shape[1])
    commands = jnp.sum(lax.all_to_all(partial_commands, "narrow", 0, 0), axis=0)
    return (slopes, commands)


def solution(mesh):
    return jax.shard_map(
        body,
        mesh=mesh,
        in_specs=(P(None, "wide", None), P(), P(None, "narrow", None), P("narrow", "wide")),
        out_specs=(P(None, "wide", None, "narrow", None), P("narrow", "wide")),
        check_vma=False,
    )
```

```python
import math

import jax
import jax.numpy as jnp
from jax import lax
from jax.sharding import PartitionSpec as P

L = 4
NSUB = 80
SAMP = 16
NPIX = 32
NSENS = 2
SPREAD = 64
FR_DEV = 4
PUP = 1280


def broadcast(block, axis, source):
    block = jnp.where(lax.axis_index(axis) == source, block, jnp.zeros_like(block))
    return lax.psum(block, axis)


def dft_table(samp, npix):
    sample_ids = jnp.arange(samp * samp, dtype=jnp.int32)
    pixel_ids = jnp.arange(npix * npix, dtype=jnp.int32)
    sample_row = sample_ids // samp
    sample_col = sample_ids % samp
    pixel_row = pixel_ids // npix - npix // 2
    pixel_col = pixel_ids % npix - npix // 2
    phase_turns = jnp.mod(
        sample_row[:, None] * pixel_row[None, :] + sample_col[:, None] * pixel_col[None, :], npix
    )
    angles = phase_turns.astype(jnp.float32) * jnp.float32(-2.0 * math.pi / npix)
    cosine = jnp.cos(angles).astype(jnp.bfloat16)
    sine_part = jnp.sin(angles).astype(jnp.bfloat16)
    top_rows = jnp.concatenate([cosine, sine_part], axis=1)
    bottom_rows = jnp.concatenate([-sine_part, cosine], axis=1)
    return jnp.concatenate([top_rows, bottom_rows], axis=0)


def subaperture_fields(pupil_phase, samp):
    sub_rows = pupil_phase.shape[0] // samp
    sub_cols = pupil_phase.shape[1] // samp
    samples = (
        pupil_phase.reshape(sub_rows, samp, sub_cols, samp)
        .transpose(0, 2, 1, 3)
        .reshape(sub_rows * sub_cols, samp * samp)
    )
    return jnp.concatenate([jnp.cos(samples), jnp.sin(samples)], axis=1).astype(jnp.bfloat16)


def centroids(fields, transform, npix):
    spectrum = jnp.dot(fields, transform, preferred_element_type=jnp.float32)
    pixel_count = npix * npix
    real_part = spectrum[:, :pixel_count]
    imag_part = spectrum[:, pixel_count:]
    intensity = real_part * real_part + imag_part * imag_part
    pixel_ids = jnp.arange(pixel_count, dtype=jnp.int32)
    along_x = (pixel_ids % npix - npix // 2).astype(jnp.float32)
    along_y = (pixel_ids // npix - npix // 2).astype(jnp.float32)
    flux_total = jnp.sum(intensity, axis=1)
    centre_x = jnp.sum(intensity * along_x[None, :], axis=1) / flux_total
    centre_y = jnp.sum(intensity * along_y[None, :], axis=1) / flux_total
    return jnp.stack([centre_x, centre_y], axis=1)


def body(screens, offsets, valid, recon):
    wide_count = lax.axis_size("wide")
    narrow_count = lax.axis_size("narrow")
    wide_index = lax.axis_index("wide")
    narrow_index = lax.axis_index("narrow")
    band_rows = screens.shape[1]
    sub_rows = valid.shape[1]
    pixel_rows = sub_rows * SAMP
    slab_rows = pixel_rows + SPREAD
    union_cols = PUP + SPREAD
    local_items = FR_DEV * NSENS
    own_offsets = lax.dynamic_slice_in_dim(offsets, wide_index * local_items, local_items, 1)
    lowest = jnp.min(offsets, axis=1)
    pad = jnp.zeros((slab_rows, union_cols), screens.dtype)
    slabs = []
    for which_layer in range(L):
        band = lax.dynamic_slice_in_dim(screens[which_layer], lowest[1, which_layer], union_cols, 1)
        padded = jnp.concatenate([pad, band, pad], axis=0)
        group_start = lowest[0, which_layer] + pixel_rows * narrow_index
        row_at = jnp.clip(group_start - wide_index * band_rows + slab_rows, 0, band_rows + slab_rows)
        slabs.append(lax.dynamic_slice_in_dim(padded, row_at, slab_rows, 0))
    slabs = jnp.stack(slabs).reshape(wide_count, L * slab_rows // wide_count, union_cols)
    slabs = jnp.sum(lax.all_to_all(slabs, "wide", 0, 0), axis=0, dtype=slabs.dtype)
    slabs = jnp.broadcast_to(slabs[None], (wide_count,) + slabs.shape)
    slabs = lax.all_to_all(slabs, "wide", 0, 0).reshape(L, slab_rows, union_cols)
    rel = own_offsets - lowest[:, None, :]
    phases = []
    for item in range(local_items):
        acc = jnp.zeros((pixel_rows, PUP), jnp.float32)
        for which_layer in range(L):
            window = lax.dynamic_slice(
                slabs[which_layer], (rel[0, item, which_layer], rel[1, item, which_layer]), (pixel_rows, PUP)
            )
            acc = acc + window.astype(jnp.float32)
        phases.append(acc)
    pupil_phase = jnp.stack(phases)
    transform = dft_table(SAMP, NPIX)
    frame_phase = pupil_phase.reshape(FR_DEV, NSENS, pixel_rows, PUP)
    valid_flags = valid.reshape(-1)

    def frame_fields(frame_block):
        return jnp.concatenate(
            [subaperture_fields(frame_block[sensor_index], SAMP) for sensor_index in range(NSENS)],
            axis=0,
        )

    def one_frame(frame_block):
        return centroids(frame_fields(frame_block), transform, NPIX) * valid_flags[:, None].astype(
            jnp.float32
        )

    measured = lax.map(one_frame, frame_phase)
    measured = measured.reshape(FR_DEV, NSENS, sub_rows, NSUB, 2)
    slopes = measured.transpose(4, 0, 1, 2, 3)
    slope_vector = (
        measured.transpose(0, 2, 1, 3, 4)
        .reshape(FR_DEV, sub_rows * NSENS * NSUB * 2)
        .astype(jnp.bfloat16)
    )
    partial_commands = jnp.dot(
        lax.all_gather(slope_vector, "wide", axis=0, tiled=True),
        recon,
        preferred_element_type=jnp.float32,
    )
    partial_commands = partial_commands.reshape(narrow_count, -1, partial_commands.shape[1])
    commands = jnp.sum(lax.all_to_all(partial_commands, "narrow", 0, 0), axis=0)
    return (slopes, commands)


def solution(mesh):
    return jax.shard_map(
        body,
        mesh=mesh,
        in_specs=(P(None, "wide", None), P(), P(None, "narrow", None), P("narrow", "wide")),
        out_specs=(P(None, "wide", None, "narrow", None), P("narrow", "wide")),
        check_vma=False,
    )
```

```python
import math

import jax
import jax.numpy as jnp
from jax import lax
from jax.sharding import PartitionSpec as P

L = 4
NSUB = 80
SAMP = 16
NPIX = 32
NSENS = 2
SPREAD = 64
FR_DEV = 4
PUP = 1280


def broadcast(block, axis, source):
    block = jnp.where(lax.axis_index(axis) == source, block, jnp.zeros_like(block))
    return lax.psum(block, axis)


def dft_table(samp, npix):
    sample_ids = jnp.arange(samp * samp, dtype=jnp.int32)
    pixel_ids = jnp.arange(npix * npix, dtype=jnp.int32)
    sample_row = sample_ids // samp
    sample_col = sample_ids % samp
    pixel_row = pixel_ids // npix - npix // 2
    pixel_col = pixel_ids % npix - npix // 2
    phase_turns = jnp.mod(
        sample_row[:, None] * pixel_row[None, :] + sample_col[:, None] * pixel_col[None, :], npix
    )
    angles = phase_turns.astype(jnp.float32) * jnp.float32(-2.0 * math.pi / npix)
    cosine = jnp.cos(angles).astype(jnp.bfloat16)
    sine_part = jnp.sin(angles).astype(jnp.bfloat16)
    top_rows = jnp.concatenate([cosine, sine_part], axis=1)
    bottom_rows = jnp.concatenate([-sine_part, cosine], axis=1)
    return jnp.concatenate([top_rows, bottom_rows], axis=0)


def subaperture_fields(pupil_phase, samp):
    sub_rows = pupil_phase.shape[0] // samp
    sub_cols = pupil_phase.shape[1] // samp
    samples = (
        pupil_phase.reshape(sub_rows, samp, sub_cols, samp)
        .transpose(0, 2, 1, 3)
        .reshape(sub_rows * sub_cols, samp * samp)
    )
    return jnp.concatenate([jnp.cos(samples), jnp.sin(samples)], axis=1).astype(jnp.bfloat16)


def centroids(fields, transform, npix):
    spectrum = jnp.dot(fields, transform, preferred_element_type=jnp.float32)
    pixel_count = npix * npix
    real_part = spectrum[:, :pixel_count]
    imag_part = spectrum[:, pixel_count:]
    intensity = real_part * real_part + imag_part * imag_part
    pixel_ids = jnp.arange(pixel_count, dtype=jnp.int32)
    along_x = (pixel_ids % npix - npix // 2).astype(jnp.float32)
    along_y = (pixel_ids // npix - npix // 2).astype(jnp.float32)
    flux_total = jnp.sum(intensity, axis=1)
    centre_x = jnp.sum(intensity * along_x[None, :], axis=1) / flux_total
    centre_y = jnp.sum(intensity * along_y[None, :], axis=1) / flux_total
    return jnp.stack([centre_x, centre_y], axis=1)


def body(screens, offsets, valid, recon):
    narrow_count = lax.axis_size("narrow")
    wide_index = lax.axis_index("wide")
    narrow_index = lax.axis_index("narrow")
    band_rows = screens.shape[1]
    sub_rows = valid.shape[1]
    pixel_rows = sub_rows * SAMP
    slab_rows = pixel_rows + SPREAD
    union_cols = PUP + SPREAD
    local_items = FR_DEV * NSENS
    own_offsets = lax.dynamic_slice_in_dim(offsets, wide_index * local_items, local_items, 1)
    lowest = jnp.min(offsets, axis=1)
    pad = jnp.zeros((slab_rows, union_cols), screens.dtype)
    slabs = []
    for which_layer in range(L):
        band = lax.dynamic_slice_in_dim(screens[which_layer], lowest[1, which_layer], union_cols, 1)
        padded = jnp.concatenate([pad, band, pad], axis=0)
        group_start = lowest[0, which_layer] + pixel_rows * narrow_index
        row_at = jnp.clip(group_start - wide_index * band_rows + slab_rows, 0, band_rows + slab_rows)
        slabs.append(lax.dynamic_slice_in_dim(padded, row_at, slab_rows, 0))
    slabs = lax.psum(jnp.stack(slabs), "wide")
    rel = own_offsets - lowest[:, None, :]
    phases = []
    for item in range(local_items):
        acc = jnp.zeros((pixel_rows, PUP), jnp.float32)
        for which_layer in range(L):
            window = lax.dynamic_slice(
                slabs[which_layer], (rel[0, item, which_layer], rel[1, item, which_layer]), (pixel_rows, PUP)
            )
            acc = acc + window.astype(jnp.float32)
        phases.append(acc)
    pupil_phase = jnp.stack(phases)
    transform = dft_table(SAMP, NPIX)
    frame_phase = pupil_phase.reshape(FR_DEV, NSENS, pixel_rows, PUP)
    valid_flags = valid.reshape(-1)

    def frame_fields(frame_block):
        return jnp.concatenate(
            [subaperture_fields(frame_block[sensor_index], SAMP) for sensor_index in range(NSENS)],
            axis=0,
        )

    def one_frame(frame_block):
        return centroids(frame_fields(frame_block), transform, NPIX) * valid_flags[:, None].astype(
            jnp.float32
        )

    measured = lax.map(one_frame, frame_phase)
    measured = measured.reshape(FR_DEV, NSENS, sub_rows, NSUB, 2)
    slopes = measured.transpose(4, 0, 1, 2, 3)
    slope_vector = (
        measured.transpose(0, 2, 1, 3, 4)
        .reshape(FR_DEV, sub_rows * NSENS * NSUB * 2)
        .astype(jnp.bfloat16)
    )
    partial_commands = jnp.dot(
        lax.all_gather(slope_vector, "wide", axis=0, tiled=True),
        recon,
        preferred_element_type=jnp.float32,
    )
    partial_commands = partial_commands.reshape(narrow_count, -1, partial_commands.shape[1])
    commands = jnp.sum(lax.all_to_all(partial_commands, "narrow", 0, 0), axis=0)
    return (slopes, commands)


def solution(mesh):
    return jax.shard_map(
        body,
        mesh=mesh,
        in_specs=(P(None, "wide", None), P(), P(None, "narrow", None), P("narrow", "wide")),
        out_specs=(P(None, "wide", None, "narrow", None), P("narrow", "wide")),
        check_vma=False,
    )
```

```python
import math

import jax
import jax.numpy as jnp
from jax import lax
from jax.sharding import PartitionSpec as P

L = 4
NSUB = 80
SAMP = 16
NPIX = 32
NSENS = 2
SPREAD = 64
FR_DEV = 4
PUP = 1280
f32 = jnp.float32
bf16 = jnp.bfloat16


def split_hi_lo(x):
    hi = x.astype(bf16)
    return hi, (x - hi.astype(f32)).astype(bf16)

def dft_factors(samp, npix):
    ids = jnp.arange(samp, dtype=jnp.int32)
    pix = jnp.arange(npix, dtype=jnp.int32) - npix // 2
    turns = jnp.mod(pix[:, None] * ids[None, :], npix)
    angles = turns.astype(f32) * f32(-2.0 * math.pi / npix)
    return jnp.cos(angles), jnp.sin(angles)

def block_diag(block, count):
    eye = jnp.eye(count, dtype=block.dtype)
    p, q = block.shape
    return (eye[:, None, :, None] * block[None, :, None, :]).reshape(count * p, count * q)

def centroids_sep(phase, sub_rows):
    items = phase.shape[0]
    rows = sub_rows * SAMP
    lane_subs = 128 // SAMP
    groups = PUP // 128
    cosf, sinf = dft_factors(SAMP, NPIX)
    bc = block_diag(cosf.T, lane_subs)
    bs = block_diag(sinf.T, lane_subs)
    rhs1 = jnp.concatenate([jnp.concatenate([bc, bs], 1), jnp.concatenate([-bs, bc], 1)], 0)
    r1_hi, r1_lo = split_hi_lo(rhs1)
    rhs1 = jnp.concatenate([r1_hi, r1_lo], 0)
    fc = jnp.cos(phase).astype(bf16).reshape(items, rows, groups, 128)
    fs = jnp.sin(phase).astype(bf16).reshape(items, rows, groups, 128)
    lhs1 = jnp.concatenate([fc, fs, fc, fs], axis=-1)
    t = jnp.einsum("irgk,kn->irgn", lhs1, rhs1, preferred_element_type=f32)
    half = lane_subs * NPIX
    tcomb = jnp.concatenate([t[..., :half], t[..., half:]], axis=1).reshape(items, 2 * rows, groups * half)
    t_hi, t_lo = split_hi_lo(tcomb)
    rhs2 = jnp.concatenate([t_hi, t_lo, t_hi], axis=1)
    ac = block_diag(cosf, sub_rows)
    as_ = block_diag(sinf, sub_rows)
    m2 = jnp.concatenate([jnp.concatenate([ac, -as_], 1), jnp.concatenate([as_, ac], 1)], 0)
    m_hi, m_lo = split_hi_lo(m2)
    lhs2 = jnp.concatenate([m_hi, m_hi, m_lo], axis=1)
    s = jnp.einsum("pq,iqn->ipn", lhs2, rhs2, preferred_element_type=f32)
    s_re = s[:, : sub_rows * NPIX]
    s_im = s[:, sub_rows * NPIX :]
    inten = (s_re * s_re + s_im * s_im).reshape(items, sub_rows, NPIX, PUP // SAMP, NPIX)
    w = jnp.arange(NPIX, dtype=f32) - NPIX // 2
    flux = jnp.sum(inten, axis=(2, 4))
    cx = jnp.sum(inten * w, axis=(2, 4)) / flux
    cy = jnp.sum(inten * w[:, None, None], axis=(2, 4)) / flux
    return jnp.stack([cx, cy], axis=-1)


def body(screens, offsets, valid, recon):
    narrow_count = lax.axis_size("narrow")
    wide_index = lax.axis_index("wide")
    narrow_index = lax.axis_index("narrow")
    band_rows = screens.shape[1]
    sub_rows = valid.shape[1]
    pixel_rows = sub_rows * SAMP
    slab_rows = pixel_rows + SPREAD
    union_cols = PUP + SPREAD
    local_items = FR_DEV * NSENS
    own_offsets = lax.dynamic_slice_in_dim(offsets, wide_index * local_items, local_items, 1)
    lowest = jnp.min(offsets, axis=1)
    pad = jnp.zeros((slab_rows, union_cols), screens.dtype)
    slabs = []
    for which_layer in range(L):
        band = lax.dynamic_slice_in_dim(screens[which_layer], lowest[1, which_layer], union_cols, 1)
        padded = jnp.concatenate([pad, band, pad], axis=0)
        group_start = lowest[0, which_layer] + pixel_rows * narrow_index
        row_at = jnp.clip(group_start - wide_index * band_rows + slab_rows, 0, band_rows + slab_rows)
        slabs.append(lax.dynamic_slice_in_dim(padded, row_at, slab_rows, 0))
    slabs = lax.psum(jnp.stack(slabs), "wide")
    rel = own_offsets - lowest[:, None, :]
    phases = []
    for item in range(local_items):
        acc = jnp.zeros((pixel_rows, PUP), jnp.float32)
        for which_layer in range(L):
            window = lax.dynamic_slice(
                slabs[which_layer], (rel[0, item, which_layer], rel[1, item, which_layer]), (pixel_rows, PUP)
            )
            acc = acc + window.astype(jnp.float32)
        phases.append(acc)
    pupil_phase = jnp.stack(phases)
    measured = centroids_sep(pupil_phase, sub_rows)
    measured = measured.reshape(FR_DEV, NSENS, sub_rows, NSUB, 2) * valid[None, :, :, :, None].astype(
        jnp.float32
    )
    slopes = measured.transpose(4, 0, 1, 2, 3)
    slope_vector = (
        measured.transpose(0, 2, 1, 3, 4)
        .reshape(FR_DEV, sub_rows * NSENS * NSUB * 2)
        .astype(jnp.bfloat16)
    )
    partial_commands = jnp.dot(
        lax.all_gather(slope_vector, "wide", axis=0, tiled=True),
        recon,
        preferred_element_type=jnp.float32,
    )
    partial_commands = partial_commands.reshape(narrow_count, -1, partial_commands.shape[1])
    commands = jnp.sum(lax.all_to_all(partial_commands, "narrow", 0, 0), axis=0)
    return (slopes, commands)


def solution(mesh):
    return jax.shard_map(
        body,
        mesh=mesh,
        in_specs=(P(None, "wide", None), P(), P(None, "narrow", None), P("narrow", "wide")),
        out_specs=(P(None, "wide", None, "narrow", None), P("narrow", "wide")),
        check_vma=False,
    )
```

```python
import math

import jax
import jax.numpy as jnp
from jax import lax
from jax.experimental import pallas as pl
from jax.sharding import PartitionSpec as P

L = 4
NSUB = 80
SAMP = 16
NPIX = 32
NSENS = 2
SPREAD = 64
FR_DEV = 4
PUP = 1280
LANES = 128
f32 = jnp.float32
bf16 = jnp.bfloat16


def split_hi_lo(x):
    hi = lax.reduce_precision(x, exponent_bits=8, mantissa_bits=7)
    return hi.astype(bf16), (x - hi).astype(bf16)


def dft_factors(samp, npix):
    ids = jnp.arange(samp, dtype=jnp.int32)
    pix = jnp.arange(npix, dtype=jnp.int32) - npix // 2
    turns = jnp.mod(pix[:, None] * ids[None, :], npix)
    angles = turns.astype(f32) * f32(-2.0 * math.pi / npix)
    return jnp.cos(angles), jnp.sin(angles)


def block_diag(block, count):
    eye = jnp.eye(count, dtype=block.dtype)
    p, q = block.shape
    return (eye[:, None, :, None] * block[None, :, None, :]).reshape(count * p, count * q)


def dft_operands(sub_rows):
    lane_subs = LANES // SAMP
    cosf, sinf = dft_factors(SAMP, NPIX)
    bc = block_diag(cosf.T, lane_subs)
    bs = block_diag(sinf.T, lane_subs)
    rhs1 = jnp.concatenate([jnp.concatenate([bc, bs], 1), jnp.concatenate([-bs, bc], 1)], 0)
    r1_hi, r1_lo = split_hi_lo(rhs1)
    rhs1 = jnp.concatenate([r1_hi, r1_lo], 0)
    ac = block_diag(cosf, sub_rows)
    as_ = block_diag(sinf, sub_rows)
    m2 = jnp.concatenate([jnp.concatenate([ac, -as_], 1), jnp.concatenate([as_, ac], 1)], 0)
    m_hi, m_lo = split_hi_lo(m2)
    lhs2 = jnp.concatenate([m_hi, m_hi, m_lo], axis=1)
    weights = jnp.arange(NPIX, dtype=f32) - NPIX // 2
    ones = jnp.ones((NPIX,), f32)
    eye_r = jnp.eye(sub_rows, dtype=f32)
    wj = jnp.concatenate([(eye_r[:, :, None] * ones).reshape(sub_rows, -1),
                          (eye_r[:, :, None] * weights).reshape(sub_rows, -1)], 0)
    wj = jnp.pad(wj, ((0, 16 - 2 * sub_rows), (0, 0))).astype(bf16)
    eye_c = jnp.eye(lane_subs, dtype=f32)
    wk = jnp.concatenate([(eye_c[:, None, :] * ones[None, :, None]).reshape(-1, lane_subs),
                          (eye_c[:, None, :] * weights[None, :, None]).reshape(-1, lane_subs)], 1)
    return rhs1, lhs2, wj, wk.astype(bf16)


def centroid_kernel(phase_ref, rhs1_ref, lhs2_ref, wj_ref, wk_ref, out_ref):
    ph = phase_ref[0]
    fc = jnp.cos(ph).astype(bf16)
    fs = jnp.sin(ph).astype(bf16)
    rhs1 = rhs1_ref[...]
    lhs2 = lhs2_ref[...]
    wj = wj_ref[...]
    wk = wk_ref[...]
    rows = ph.shape[0]
    half = rhs1.shape[1] // 2
    for g in range(ph.shape[1] // LANES):
        fcg = fc[:, g * LANES:(g + 1) * LANES]
        fsg = fs[:, g * LANES:(g + 1) * LANES]
        lhs = jnp.concatenate([fcg, fsg, fcg, fsg], axis=1)
        t = jnp.dot(lhs, rhs1, preferred_element_type=f32)
        tc = jnp.concatenate([t[:, :half], t[:, half:]], axis=0)
        t_hi = tc.astype(bf16)
        t_lo = (tc - t_hi.astype(f32)).astype(bf16)
        s = jnp.dot(lhs2, jnp.concatenate([t_hi, t_lo, t_hi], axis=0), preferred_element_type=f32)
        sr = s[:rows * 2]
        si = s[rows * 2:]
        inten = sr * sr + si * si
        i_hi = inten.astype(bf16)
        i_lo = (inten - i_hi.astype(f32)).astype(bf16)
        pj = jnp.dot(wj, i_hi, preferred_element_type=f32) + jnp.dot(wj, i_lo, preferred_element_type=f32)
        p_hi = pj.astype(bf16)
        p_lo = (pj - p_hi.astype(f32)).astype(bf16)
        q = jnp.dot(p_hi, wk, preferred_element_type=f32) + jnp.dot(p_lo, wk, preferred_element_type=f32)
        out_ref[0, g] = q


def centroids_kernel(phase, sub_rows):
    items, rows, cols = phase.shape
    groups = cols // LANES
    rhs1, lhs2, wj, wk = dft_operands(sub_rows)
    sums = pl.pallas_call(
        centroid_kernel,
        grid=(items,),
        in_specs=[
            pl.BlockSpec((1, rows, cols), lambda i: (i, 0, 0)),
            pl.BlockSpec(rhs1.shape, lambda i: (0, 0)),
            pl.BlockSpec(lhs2.shape, lambda i: (0, 0)),
            pl.BlockSpec(wj.shape, lambda i: (0, 0)),
            pl.BlockSpec(wk.shape, lambda i: (0, 0)),
        ],
        out_specs=pl.BlockSpec((1, groups, 16, 16), lambda i: (i, 0, 0, 0)),
        out_shape=jax.ShapeDtypeStruct((items, groups, 16, 16), f32),
    )(phase, rhs1, lhs2, wj, wk)
    lane_subs = LANES // SAMP
    sums = sums.transpose(0, 2, 1, 3)
    flux = sums[:, :sub_rows, :, :lane_subs].reshape(items, sub_rows, -1)
    sum_x = sums[:, :sub_rows, :, lane_subs:2 * lane_subs].reshape(items, sub_rows, -1)
    sum_y = sums[:, sub_rows:2 * sub_rows, :, :lane_subs].reshape(items, sub_rows, -1)
    return jnp.stack([sum_x / flux, sum_y / flux], axis=-1)


def body(screens, offsets, valid, recon):
    narrow_count = lax.axis_size("narrow")
    wide_index = lax.axis_index("wide")
    narrow_index = lax.axis_index("narrow")
    band_rows = screens.shape[1]
    sub_rows = valid.shape[1]
    pixel_rows = sub_rows * SAMP
    slab_rows = pixel_rows + SPREAD
    union_cols = PUP + SPREAD
    local_items = FR_DEV * NSENS
    own_offsets = lax.dynamic_slice_in_dim(offsets, wide_index * local_items, local_items, 1)
    lowest = jnp.min(offsets, axis=1)
    pad = jnp.zeros((slab_rows, union_cols), screens.dtype)
    slabs = []
    for which_layer in range(L):
        band = lax.dynamic_slice_in_dim(screens[which_layer], lowest[1, which_layer], union_cols, 1)
        padded = jnp.concatenate([pad, band, pad], axis=0)
        group_start = lowest[0, which_layer] + pixel_rows * narrow_index
        row_at = jnp.clip(group_start - wide_index * band_rows + slab_rows, 0, band_rows + slab_rows)
        slabs.append(lax.dynamic_slice_in_dim(padded, row_at, slab_rows, 0))
    slabs = lax.psum(jnp.stack(slabs), "wide")
    rel = own_offsets - lowest[:, None, :]
    phases = []
    for item in range(local_items):
        acc = jnp.zeros((pixel_rows, PUP), jnp.float32)
        for which_layer in range(L):
            window = lax.dynamic_slice(
                slabs[which_layer], (rel[0, item, which_layer], rel[1, item, which_layer]), (pixel_rows, PUP)
            )
            acc = acc + window.astype(jnp.float32)
        phases.append(acc)
    pupil_phase = jnp.stack(phases)
    measured = centroids_kernel(pupil_phase, sub_rows)
    measured = measured.reshape(FR_DEV, NSENS, sub_rows, NSUB, 2) * valid[None, :, :, :, None].astype(
        jnp.float32
    )
    slopes = measured.transpose(4, 0, 1, 2, 3)
    slope_vector = (
        measured.transpose(0, 2, 1, 3, 4)
        .reshape(FR_DEV, sub_rows * NSENS * NSUB * 2)
        .astype(jnp.bfloat16)
    )
    partial_commands = jnp.dot(
        lax.all_gather(slope_vector, "wide", axis=0, tiled=True),
        recon,
        preferred_element_type=jnp.float32,
    )
    partial_commands = partial_commands.reshape(narrow_count, -1, partial_commands.shape[1])
    commands = jnp.sum(lax.all_to_all(partial_commands, "narrow", 0, 0), axis=0)
    return (slopes, commands)


def solution(mesh):
    return jax.shard_map(
        body,
        mesh=mesh,
        in_specs=(P(None, "wide", None), P(), P(None, "narrow", None), P("narrow", "wide")),
        out_specs=(P(None, "wide", None, "narrow", None), P("narrow", "wide")),
        check_vma=False,
    )
```

```python
import math

import jax
import jax.numpy as jnp
from jax import lax
from jax.experimental import pallas as pl
from jax.experimental.pallas import tpu as pltpu
from jax.sharding import PartitionSpec as P

L = 4
NSUB = 80
SAMP = 16
NPIX = 32
NSENS = 2
SPREAD = 64
FR_DEV = 4
PUP = 1280
LANES = 128
f32 = jnp.float32
bf16 = jnp.bfloat16


def split_hi_lo(x):
    hi = lax.reduce_precision(x, exponent_bits=8, mantissa_bits=7)
    return hi.astype(bf16), (x - hi).astype(bf16)


def dft_factors(samp, npix):
    ids = jnp.arange(samp, dtype=jnp.int32)
    pix = jnp.arange(npix, dtype=jnp.int32) - npix // 2
    turns = jnp.mod(pix[:, None] * ids[None, :], npix)
    angles = turns.astype(f32) * f32(-2.0 * math.pi / npix)
    return jnp.cos(angles), jnp.sin(angles)


def block_diag(block, count):
    eye = jnp.eye(count, dtype=block.dtype)
    p, q = block.shape
    return (eye[:, None, :, None] * block[None, :, None, :]).reshape(count * p, count * q)


def dft_operands(sub_rows):
    lane_subs = LANES // SAMP
    cosf, sinf = dft_factors(SAMP, NPIX)
    bc = block_diag(cosf.T, lane_subs)
    bs = block_diag(sinf.T, lane_subs)
    rhs1 = jnp.concatenate([jnp.concatenate([bc, bs], 1), jnp.concatenate([-bs, bc], 1)], 0)
    r1_hi, r1_lo = split_hi_lo(rhs1)
    rhs1 = jnp.concatenate([r1_hi, r1_lo], 0)
    ac = block_diag(cosf, sub_rows)
    as_ = block_diag(sinf, sub_rows)
    m2 = jnp.concatenate([jnp.concatenate([ac, -as_], 1), jnp.concatenate([as_, ac], 1)], 0)
    m_hi, m_lo = split_hi_lo(m2)
    lhs2 = jnp.concatenate([m_hi, m_hi, m_lo], axis=1)
    weights = jnp.arange(NPIX, dtype=f32) - NPIX // 2
    ones = jnp.ones((NPIX,), f32)
    eye_c = jnp.eye(lane_subs, dtype=f32)
    wk = jnp.concatenate([(eye_c[:, None, :] * ones[None, :, None]).reshape(-1, lane_subs),
                          (eye_c[:, None, :] * weights[None, :, None]).reshape(-1, lane_subs)], 1)
    return rhs1, lhs2, wk.astype(bf16)


def centroid_kernel(phase_ref, rhs1_ref, lhs2_ref, wk_ref, out_ref, acc_ref):
    ph = phase_ref[0]
    fc = jnp.cos(ph).astype(bf16)
    fs = jnp.sin(ph).astype(bf16)
    rhs1 = rhs1_ref[...]
    lhs2 = lhs2_ref[...]
    wk = wk_ref[...]
    rows = ph.shape[0]
    sub_rows = rows // SAMP
    groups = ph.shape[1] // LANES
    half = rhs1.shape[1] // 2
    lhs = jnp.concatenate(
        [
            jnp.concatenate([fc[:, g * LANES:(g + 1) * LANES], fs[:, g * LANES:(g + 1) * LANES]] * 2, axis=1)
            for g in range(groups)
        ],
        axis=0,
    )
    t_all = jnp.dot(lhs, rhs1, preferred_element_type=f32)
    weights = (lax.broadcasted_iota(jnp.int32, (sub_rows, NPIX, 2 * half), 1) - NPIX // 2).astype(f32)
    for g in range(groups):
        t = t_all[g * rows:(g + 1) * rows]
        tc = jnp.concatenate([t[:, :half], t[:, half:]], axis=0)
        t_hi = tc.astype(bf16)
        t_lo = (tc - t_hi.astype(f32)).astype(bf16)
        s = jnp.dot(lhs2, jnp.concatenate([t_hi, t_lo, t_hi], axis=0), preferred_element_type=f32)
        sr = s[:rows * 2]
        si = s[rows * 2:]
        inten = (sr * sr + si * si).reshape(sub_rows, NPIX, half)
        acc_ref[g, 0:sub_rows, :] = jnp.sum(inten, axis=1)
        acc_ref[g, sub_rows:2 * sub_rows, :] = jnp.sum(inten * weights[:, :, :half], axis=1)
        acc_ref[g, 2 * sub_rows:, :] = jnp.zeros((acc_ref.shape[1] - 2 * sub_rows, half), f32)
    pj = acc_ref[...].reshape(groups * acc_ref.shape[1], half)
    p_hi = pj.astype(bf16)
    p_lo = (pj - p_hi.astype(f32)).astype(bf16)
    q = jnp.dot(p_hi, wk, preferred_element_type=f32) + jnp.dot(p_lo, wk, preferred_element_type=f32)
    out_ref[0] = q.reshape(groups, acc_ref.shape[1], wk.shape[1])


def centroids_kernel(phase, sub_rows):
    items, rows, cols = phase.shape
    groups = cols // LANES
    rhs1, lhs2, wk = dft_operands(sub_rows)
    sums = pl.pallas_call(
        centroid_kernel,
        grid=(items,),
        in_specs=[
            pl.BlockSpec((1, rows, cols), lambda i: (i, 0, 0)),
            pl.BlockSpec(rhs1.shape, lambda i: (0, 0)),
            pl.BlockSpec(lhs2.shape, lambda i: (0, 0)),
            pl.BlockSpec(wk.shape, lambda i: (0, 0)),
        ],
        out_specs=pl.BlockSpec((1, groups, 16, 16), lambda i: (i, 0, 0, 0)),
        out_shape=jax.ShapeDtypeStruct((items, groups, 16, 16), f32),
        scratch_shapes=[pltpu.VMEM((groups, 16, rhs1.shape[1] // 2), f32)],
    )(phase, rhs1, lhs2, wk)
    lane_subs = LANES // SAMP
    sums = sums.transpose(0, 2, 1, 3)
    flux = sums[:, :sub_rows, :, :lane_subs].reshape(items, sub_rows, -1)
    sum_x = sums[:, :sub_rows, :, lane_subs:2 * lane_subs].reshape(items, sub_rows, -1)
    sum_y = sums[:, sub_rows:2 * sub_rows, :, :lane_subs].reshape(items, sub_rows, -1)
    return jnp.stack([sum_x / flux, sum_y / flux], axis=-1)


def body(screens, offsets, valid, recon):
    narrow_count = lax.axis_size("narrow")
    wide_index = lax.axis_index("wide")
    narrow_index = lax.axis_index("narrow")
    band_rows = screens.shape[1]
    sub_rows = valid.shape[1]
    pixel_rows = sub_rows * SAMP
    slab_rows = pixel_rows + SPREAD
    union_cols = PUP + SPREAD
    local_items = FR_DEV * NSENS
    own_offsets = lax.dynamic_slice_in_dim(offsets, wide_index * local_items, local_items, 1)
    lowest = jnp.min(offsets, axis=1)
    pad = jnp.zeros((slab_rows, union_cols), screens.dtype)
    slabs = []
    for which_layer in range(L):
        band = lax.dynamic_slice_in_dim(screens[which_layer], lowest[1, which_layer], union_cols, 1)
        padded = jnp.concatenate([pad, band, pad], axis=0)
        group_start = lowest[0, which_layer] + pixel_rows * narrow_index
        row_at = jnp.clip(group_start - wide_index * band_rows + slab_rows, 0, band_rows + slab_rows)
        slabs.append(lax.dynamic_slice_in_dim(padded, row_at, slab_rows, 0))
    slabs = lax.psum(jnp.stack(slabs), "wide")
    rel = own_offsets - lowest[:, None, :]
    phases = []
    for item in range(local_items):
        acc = jnp.zeros((pixel_rows, PUP), jnp.float32)
        for which_layer in range(L):
            window = lax.dynamic_slice(
                slabs[which_layer], (rel[0, item, which_layer], rel[1, item, which_layer]), (pixel_rows, PUP)
            )
            acc = acc + window.astype(jnp.float32)
        phases.append(acc)
    pupil_phase = jnp.stack(phases)
    measured = centroids_kernel(pupil_phase, sub_rows)
    measured = measured.reshape(FR_DEV, NSENS, sub_rows, NSUB, 2) * valid[None, :, :, :, None].astype(
        jnp.float32
    )
    slopes = measured.transpose(4, 0, 1, 2, 3)
    slope_vector = (
        measured.transpose(0, 2, 1, 3, 4)
        .reshape(FR_DEV, sub_rows * NSENS * NSUB * 2)
        .astype(jnp.bfloat16)
    )
    partial_commands = jnp.dot(
        lax.all_gather(slope_vector, "wide", axis=0, tiled=True),
        recon,
        preferred_element_type=jnp.float32,
    )
    partial_commands = partial_commands.reshape(narrow_count, -1, partial_commands.shape[1])
    commands = jnp.sum(lax.all_to_all(partial_commands, "narrow", 0, 0), axis=0)
    return (slopes, commands)


def solution(mesh):
    return jax.shard_map(
        body,
        mesh=mesh,
        in_specs=(P(None, "wide", None), P(), P(None, "narrow", None), P("narrow", "wide")),
        out_specs=(P(None, "wide", None, "narrow", None), P("narrow", "wide")),
        check_vma=False,
    )
```

```python
import math

import jax
import jax.numpy as jnp
from jax import lax
from jax.experimental import pallas as pl
from jax.experimental.pallas import tpu as pltpu
from jax.sharding import PartitionSpec as P

L = 4
NSUB = 80
SAMP = 16
NPIX = 32
NSENS = 2
SPREAD = 64
FR_DEV = 4
PUP = 1280
LANES = 128
f32 = jnp.float32
bf16 = jnp.bfloat16


def split_hi_lo(x):
    hi = lax.reduce_precision(x, exponent_bits=8, mantissa_bits=7)
    return hi.astype(bf16), (x - hi).astype(bf16)


def dft_factors(samp, npix):
    ids = jnp.arange(samp, dtype=jnp.int32)
    pix = jnp.arange(npix, dtype=jnp.int32) - npix // 2
    turns = jnp.mod(pix[:, None] * ids[None, :], npix)
    angles = turns.astype(f32) * f32(-2.0 * math.pi / npix)
    return jnp.cos(angles), jnp.sin(angles)


def block_diag(block, count):
    eye = jnp.eye(count, dtype=block.dtype)
    p, q = block.shape
    return (eye[:, None, :, None] * block[None, :, None, :]).reshape(count * p, count * q)


def dft_operands(sub_rows):
    lane_subs = LANES // SAMP
    cosf, sinf = dft_factors(SAMP, NPIX)
    bc = block_diag(cosf.T, lane_subs)
    bs = block_diag(sinf.T, lane_subs)
    rhs1 = jnp.concatenate([jnp.concatenate([bc, bs], 1), jnp.concatenate([-bs, bc], 1)], 0)
    r1_hi, r1_lo = split_hi_lo(rhs1)
    rhs1 = jnp.concatenate([r1_hi, r1_lo], 0)
    ac = block_diag(cosf, sub_rows)
    as_ = block_diag(sinf, sub_rows)
    m2 = jnp.concatenate([jnp.concatenate([ac, -as_], 1), jnp.concatenate([as_, ac], 1)], 0)
    m_hi, m_lo = split_hi_lo(m2)
    lhs2 = jnp.concatenate([m_hi, m_hi, m_lo], axis=1)
    weights = jnp.arange(NPIX, dtype=f32) - NPIX // 2
    ones = jnp.ones((NPIX,), f32)
    eye_c = jnp.eye(lane_subs, dtype=f32)
    wk = jnp.concatenate([(eye_c[:, None, :] * ones[None, :, None]).reshape(-1, lane_subs),
                          (eye_c[:, None, :] * weights[None, :, None]).reshape(-1, lane_subs)], 1)
    return rhs1, lhs2, wk.astype(bf16)


def centroid_kernel(phase_ref, rhs1_ref, lhs2_ref, wk_ref, out_ref, acc_ref):
    ph = phase_ref[0]
    fc = jnp.cos(ph).astype(bf16)
    fs = jnp.sin(ph).astype(bf16)
    rhs1 = rhs1_ref[...]
    lhs2 = lhs2_ref[...]
    wk = wk_ref[...]
    rows = ph.shape[0]
    sub_rows = rows // SAMP
    groups = ph.shape[1] // LANES
    half = rhs1.shape[1] // 2
    lhs = jnp.concatenate(
        [
            jnp.concatenate([fc[:, g * LANES:(g + 1) * LANES], fs[:, g * LANES:(g + 1) * LANES]] * 2, axis=1)
            for g in range(groups)
        ],
        axis=0,
    )
    t_all = jnp.dot(lhs, rhs1, preferred_element_type=f32)
    weights = (lax.broadcasted_iota(jnp.int32, (sub_rows, NPIX, 2 * half), 1) - NPIX // 2).astype(f32)
    for g in range(groups):
        t = t_all[g * rows:(g + 1) * rows]
        tc = jnp.concatenate([t[:, :half], t[:, half:]], axis=0)
        t_hi = tc.astype(bf16)
        t_lo = (tc - t_hi.astype(f32)).astype(bf16)
        s = jnp.dot(lhs2, jnp.concatenate([t_hi, t_lo, t_hi], axis=0), preferred_element_type=f32)
        sr = s[:rows * 2]
        si = s[rows * 2:]
        inten = (sr * sr + si * si).reshape(sub_rows, NPIX, half)
        acc_ref[g, 0:sub_rows, :] = jnp.sum(inten, axis=1)
        acc_ref[g, sub_rows:2 * sub_rows, :] = jnp.sum(inten * weights[:, :, :half], axis=1)
        acc_ref[g, 2 * sub_rows:, :] = jnp.zeros((acc_ref.shape[1] - 2 * sub_rows, half), f32)
    pj = acc_ref[...].reshape(groups * acc_ref.shape[1], half)
    p_hi = pj.astype(bf16)
    p_lo = (pj - p_hi.astype(f32)).astype(bf16)
    q = jnp.dot(p_hi, wk, preferred_element_type=f32) + jnp.dot(p_lo, wk, preferred_element_type=f32)
    out_ref[0] = q.reshape(groups, acc_ref.shape[1], wk.shape[1])


def centroids_kernel(phase, sub_rows):
    items, rows, cols = phase.shape
    groups = cols // LANES
    rhs1, lhs2, wk = dft_operands(sub_rows)
    sums = pl.pallas_call(
        centroid_kernel,
        grid=(items,),
        in_specs=[
            pl.BlockSpec((1, rows, cols), lambda i: (i, 0, 0)),
            pl.BlockSpec(rhs1.shape, lambda i: (0, 0)),
            pl.BlockSpec(lhs2.shape, lambda i: (0, 0)),
            pl.BlockSpec(wk.shape, lambda i: (0, 0)),
        ],
        out_specs=pl.BlockSpec((1, groups, 16, 16), lambda i: (i, 0, 0, 0)),
        out_shape=jax.ShapeDtypeStruct((items, groups, 16, 16), f32),
        scratch_shapes=[pltpu.VMEM((groups, 16, rhs1.shape[1] // 2), f32)],
    )(phase, rhs1, lhs2, wk)
    lane_subs = LANES // SAMP
    sums = sums.transpose(0, 2, 1, 3)
    flux = sums[:, :sub_rows, :, :lane_subs].reshape(items, sub_rows, -1)
    sum_x = sums[:, :sub_rows, :, lane_subs:2 * lane_subs].reshape(items, sub_rows, -1)
    sum_y = sums[:, sub_rows:2 * sub_rows, :, :lane_subs].reshape(items, sub_rows, -1)
    return jnp.stack([sum_x / flux, sum_y / flux], axis=-1)


def body(screens, offsets, valid, recon):
    narrow_count = lax.axis_size("narrow")
    wide_count = lax.axis_size("wide")
    wide_index = lax.axis_index("wide")
    narrow_index = lax.axis_index("narrow")
    band_rows = screens.shape[1]
    sub_rows = valid.shape[1]
    pixel_rows = sub_rows * SAMP
    slab_rows = pixel_rows + SPREAD
    union_cols = PUP + SPREAD
    local_items = FR_DEV * NSENS
    own_offsets = lax.dynamic_slice_in_dim(offsets, wide_index * local_items, local_items, 1)
    lowest = jnp.min(offsets, axis=1)
    pad = jnp.zeros((slab_rows, union_cols), screens.dtype)
    slabs = []
    for which_layer in range(L):
        band = lax.dynamic_slice_in_dim(screens[which_layer], lowest[1, which_layer], union_cols, 1)
        padded = jnp.concatenate([pad, band, pad], axis=0)
        group_start = lowest[0, which_layer] + pixel_rows * narrow_index
        row_at = jnp.clip(group_start - wide_index * band_rows + slab_rows, 0, band_rows + slab_rows)
        slabs.append(lax.dynamic_slice_in_dim(padded, row_at, slab_rows, 0))
    chunks = jnp.stack(slabs).reshape(wide_count, L * slab_rows // wide_count, union_cols)
    chunk = jnp.sum(lax.all_to_all(chunks, "wide", 0, 0), axis=0, dtype=chunks.dtype)
    gathered = [chunk]
    for shift in range(1, wide_count):
        pairs = [(source, (source + shift) % wide_count) for source in range(wide_count)]
        gathered.append(lax.ppermute(chunk, "wide", pairs))
    order = (wide_index - jnp.arange(wide_count)) % wide_count
    slabs = jnp.stack(gathered)[order].reshape(L, slab_rows, union_cols)
    rel = own_offsets - lowest[:, None, :]
    phases = []
    for item in range(local_items):
        acc = jnp.zeros((pixel_rows, PUP), jnp.float32)
        for which_layer in range(L):
            window = lax.dynamic_slice(
                slabs[which_layer], (rel[0, item, which_layer], rel[1, item, which_layer]), (pixel_rows, PUP)
            )
            acc = acc + window.astype(jnp.float32)
        phases.append(acc)
    pupil_phase = jnp.stack(phases)
    measured = centroids_kernel(pupil_phase, sub_rows)
    measured = measured.reshape(FR_DEV, NSENS, sub_rows, NSUB, 2) * valid[None, :, :, :, None].astype(
        jnp.float32
    )
    slopes = measured.transpose(4, 0, 1, 2, 3)
    slope_vector = (
        measured.transpose(0, 2, 1, 3, 4)
        .reshape(FR_DEV, sub_rows * NSENS * NSUB * 2)
        .astype(jnp.bfloat16)
    )
    partial_commands = jnp.dot(
        lax.all_gather(slope_vector, "wide", axis=0, tiled=True),
        recon,
        preferred_element_type=jnp.float32,
    )
    partial_commands = partial_commands.reshape(narrow_count, -1, partial_commands.shape[1])
    commands = jnp.sum(lax.all_to_all(partial_commands, "narrow", 0, 0), axis=0)
    return (slopes, commands)


def solution(mesh):
    return jax.shard_map(
        body,
        mesh=mesh,
        in_specs=(P(None, "wide", None), P(), P(None, "narrow", None), P("narrow", "wide")),
        out_specs=(P(None, "wide", None, "narrow", None), P("narrow", "wide")),
        check_vma=False,
    )
```

```python
import math

import jax
import jax.numpy as jnp
from jax import lax
from jax.experimental import pallas as pl
from jax.experimental.pallas import tpu as pltpu
from jax.sharding import PartitionSpec as P

L = 4
NSUB = 80
SAMP = 16
NPIX = 32
NSENS = 2
SPREAD = 64
FR_DEV = 4
PUP = 1280
LANES = 128
f32 = jnp.float32
bf16 = jnp.bfloat16


def split_hi_lo(x):
    hi = lax.reduce_precision(x, exponent_bits=8, mantissa_bits=7)
    return hi.astype(bf16), (x - hi).astype(bf16)


def dft_factors(samp, npix):
    ids = jnp.arange(samp, dtype=jnp.int32)
    pix = jnp.arange(npix, dtype=jnp.int32) - npix // 2
    turns = jnp.mod(pix[:, None] * ids[None, :], npix)
    angles = turns.astype(f32) * f32(-2.0 * math.pi / npix)
    return jnp.cos(angles), jnp.sin(angles)


def block_diag(block, count):
    eye = jnp.eye(count, dtype=block.dtype)
    p, q = block.shape
    return (eye[:, None, :, None] * block[None, :, None, :]).reshape(count * p, count * q)


def dft_operands(sub_rows):
    lane_subs = LANES // SAMP
    cosf, sinf = dft_factors(SAMP, NPIX)
    bc = block_diag(cosf.T, lane_subs)
    bs = block_diag(sinf.T, lane_subs)
    rhs1 = jnp.concatenate([jnp.concatenate([bc, bs], 1), jnp.concatenate([-bs, bc], 1)], 0)
    r1_hi, r1_lo = split_hi_lo(rhs1)
    rhs1 = jnp.concatenate([r1_hi, r1_lo], 0)
    ac = block_diag(cosf, sub_rows)
    as_ = block_diag(sinf, sub_rows)
    m2 = jnp.concatenate([jnp.concatenate([ac, -as_], 1), jnp.concatenate([as_, ac], 1)], 0)
    m_hi, m_lo = split_hi_lo(m2)
    lhs2 = jnp.concatenate([m_hi, m_hi, m_lo], axis=1)
    weights = jnp.arange(NPIX, dtype=f32) - NPIX // 2
    ones = jnp.ones((NPIX,), f32)
    eye_c = jnp.eye(lane_subs, dtype=f32)
    wk = jnp.concatenate([(eye_c[:, None, :] * ones[None, :, None]).reshape(-1, lane_subs),
                          (eye_c[:, None, :] * weights[None, :, None]).reshape(-1, lane_subs)], 1)
    return rhs1, lhs2, wk.astype(bf16)


def centroid_kernel(phase_ref, rhs1_ref, lhs2_ref, wk_ref, out_ref, acc_ref):
    ph = phase_ref[0]
    fc = jnp.cos(ph).astype(bf16)
    fs = jnp.sin(ph).astype(bf16)
    rhs1 = rhs1_ref[...]
    lhs2 = lhs2_ref[...]
    wk = wk_ref[...]
    rows = ph.shape[0]
    sub_rows = rows // SAMP
    groups = ph.shape[1] // LANES
    half = rhs1.shape[1] // 2
    lhs = jnp.concatenate(
        [
            jnp.concatenate([fc[:, g * LANES:(g + 1) * LANES], fs[:, g * LANES:(g + 1) * LANES]] * 2, axis=1)
            for g in range(groups)
        ],
        axis=0,
    )
    t_all = jnp.dot(lhs, rhs1, preferred_element_type=f32)
    weights = (lax.broadcasted_iota(jnp.int32, (sub_rows, NPIX, 2 * half), 1) - NPIX // 2).astype(f32)
    for g in range(groups):
        t = t_all[g * rows:(g + 1) * rows]
        tc = jnp.concatenate([t[:, :half], t[:, half:]], axis=0)
        t_hi = tc.astype(bf16)
        t_lo = (tc - t_hi.astype(f32)).astype(bf16)
        s = jnp.dot(lhs2, jnp.concatenate([t_hi, t_lo, t_hi], axis=0), preferred_element_type=f32)
        sr = s[:rows * 2]
        si = s[rows * 2:]
        inten = (sr * sr + si * si).reshape(sub_rows, NPIX, half)
        acc_ref[g, 0:sub_rows, :] = jnp.sum(inten, axis=1)
        acc_ref[g, sub_rows:2 * sub_rows, :] = jnp.sum(inten * weights[:, :, :half], axis=1)
        acc_ref[g, 2 * sub_rows:, :] = jnp.zeros((acc_ref.shape[1] - 2 * sub_rows, half), f32)
    pj = acc_ref[...].reshape(groups * acc_ref.shape[1], half)
    p_hi = pj.astype(bf16)
    p_lo = (pj - p_hi.astype(f32)).astype(bf16)
    q = jnp.dot(p_hi, wk, preferred_element_type=f32) + jnp.dot(p_lo, wk, preferred_element_type=f32)
    out_ref[0] = q.reshape(groups, acc_ref.shape[1], wk.shape[1])


def centroids_kernel(phase, sub_rows):
    items, rows, cols = phase.shape
    groups = cols // LANES
    rhs1, lhs2, wk = dft_operands(sub_rows)
    sums = pl.pallas_call(
        centroid_kernel,
        grid=(items,),
        in_specs=[
            pl.BlockSpec((1, rows, cols), lambda i: (i, 0, 0)),
            pl.BlockSpec(rhs1.shape, lambda i: (0, 0)),
            pl.BlockSpec(lhs2.shape, lambda i: (0, 0)),
            pl.BlockSpec(wk.shape, lambda i: (0, 0)),
        ],
        out_specs=pl.BlockSpec((1, groups, 16, 16), lambda i: (i, 0, 0, 0)),
        out_shape=jax.ShapeDtypeStruct((items, groups, 16, 16), f32),
        scratch_shapes=[pltpu.VMEM((groups, 16, rhs1.shape[1] // 2), f32)],
    )(phase, rhs1, lhs2, wk)
    lane_subs = LANES // SAMP
    sums = sums.transpose(0, 2, 1, 3)
    flux = sums[:, :sub_rows, :, :lane_subs].reshape(items, sub_rows, -1)
    sum_x = sums[:, :sub_rows, :, lane_subs:2 * lane_subs].reshape(items, sub_rows, -1)
    sum_y = sums[:, sub_rows:2 * sub_rows, :, :lane_subs].reshape(items, sub_rows, -1)
    return jnp.stack([sum_x / flux, sum_y / flux], axis=-1)


def body(screens, offsets, valid, recon):
    narrow_count = lax.axis_size("narrow")
    wide_index = lax.axis_index("wide")
    narrow_index = lax.axis_index("narrow")
    band_rows = screens.shape[1]
    sub_rows = valid.shape[1]
    pixel_rows = sub_rows * SAMP
    slab_rows = pixel_rows + SPREAD
    union_cols = PUP + SPREAD
    local_items = FR_DEV * NSENS
    own_offsets = lax.dynamic_slice_in_dim(offsets, wide_index * local_items, local_items, 1)
    lowest = jnp.min(offsets, axis=1)
    pad = jnp.zeros((slab_rows, union_cols), screens.dtype)
    slabs = []
    for which_layer in range(L):
        band = lax.dynamic_slice(
            screens, (which_layer, 0, lowest[1, which_layer]), (1, band_rows, union_cols)
        )[0]
        padded = jnp.concatenate([pad, band, pad], axis=0)
        group_start = lowest[0, which_layer] + pixel_rows * narrow_index
        row_at = jnp.clip(group_start - wide_index * band_rows + slab_rows, 0, band_rows + slab_rows)
        slabs.append(lax.dynamic_slice_in_dim(padded, row_at, slab_rows, 0))
    slabs = lax.psum(jnp.stack(slabs), "wide")
    rel = own_offsets - lowest[:, None, :]
    phases = []
    for item in range(local_items):
        acc = jnp.zeros((pixel_rows, PUP), jnp.float32)
        for which_layer in range(L):
            window = lax.dynamic_slice(
                slabs[which_layer], (rel[0, item, which_layer], rel[1, item, which_layer]), (pixel_rows, PUP)
            )
            acc = acc + window.astype(jnp.float32)
        phases.append(acc)
    pupil_phase = jnp.stack(phases)
    measured = centroids_kernel(pupil_phase, sub_rows)
    measured = measured.reshape(FR_DEV, NSENS, sub_rows, NSUB, 2) * valid[None, :, :, :, None].astype(
        jnp.float32
    )
    slopes = measured.transpose(4, 0, 1, 2, 3)
    slope_vector = (
        measured.transpose(0, 2, 1, 3, 4)
        .reshape(FR_DEV, sub_rows * NSENS * NSUB * 2)
        .astype(jnp.bfloat16)
    )
    partial_commands = jnp.dot(
        lax.all_gather(slope_vector, "wide", axis=0, tiled=True),
        recon,
        preferred_element_type=jnp.float32,
    )
    partial_commands = partial_commands.reshape(narrow_count, -1, partial_commands.shape[1])
    commands = jnp.sum(lax.all_to_all(partial_commands, "narrow", 0, 0), axis=0)
    return (slopes, commands)


def solution(mesh):
    return jax.shard_map(
        body,
        mesh=mesh,
        in_specs=(P(None, "wide", None), P(), P(None, "narrow", None), P("narrow", "wide")),
        out_specs=(P(None, "wide", None, "narrow", None), P("narrow", "wide")),
        check_vma=False,
    )
```

```python
import math

import jax
import jax.numpy as jnp
from jax import lax
from jax.experimental import pallas as pl
from jax.experimental.pallas import tpu as pltpu
from jax.sharding import PartitionSpec as P

L = 4
NSUB = 80
SAMP = 16
NPIX = 32
NSENS = 2
SPREAD = 64
FR_DEV = 4
PUP = 1280
LANES = 128
f32 = jnp.float32
bf16 = jnp.bfloat16


def split_hi_lo(x):
    hi = lax.reduce_precision(x, exponent_bits=8, mantissa_bits=7)
    return hi.astype(bf16), (x - hi).astype(bf16)


def dft_factors(samp, npix):
    ids = jnp.arange(samp, dtype=jnp.int32)
    pix = jnp.arange(npix, dtype=jnp.int32) - npix // 2
    turns = jnp.mod(pix[:, None] * ids[None, :], npix)
    angles = turns.astype(f32) * f32(-2.0 * math.pi / npix)
    return jnp.cos(angles), jnp.sin(angles)


def block_diag(block, count):
    eye = jnp.eye(count, dtype=block.dtype)
    p, q = block.shape
    return (eye[:, None, :, None] * block[None, :, None, :]).reshape(count * p, count * q)


def dft_operands(sub_rows):
    lane_subs = LANES // SAMP
    cosf, sinf = dft_factors(SAMP, NPIX)
    bc = block_diag(cosf.T, lane_subs)
    bs = block_diag(sinf.T, lane_subs)
    rhs1 = jnp.concatenate([jnp.concatenate([bc, bs], 1), jnp.concatenate([-bs, bc], 1)], 0)
    r1_hi, r1_lo = split_hi_lo(rhs1)
    rhs1 = jnp.concatenate([r1_hi, r1_lo], 0)
    ac = block_diag(cosf, sub_rows)
    as_ = block_diag(sinf, sub_rows)
    m2 = jnp.concatenate([jnp.concatenate([ac, -as_], 1), jnp.concatenate([as_, ac], 1)], 0)
    m_hi, m_lo = split_hi_lo(m2)
    lhs2 = jnp.concatenate([m_hi, m_hi, m_lo], axis=1)
    weights = jnp.arange(NPIX, dtype=f32) - NPIX // 2
    ones = jnp.ones((NPIX,), f32)
    eye_c = jnp.eye(lane_subs, dtype=f32)
    wk = jnp.concatenate([(eye_c[:, None, :] * ones[None, :, None]).reshape(-1, lane_subs),
                          (eye_c[:, None, :] * weights[None, :, None]).reshape(-1, lane_subs)], 1)
    return rhs1, lhs2, wk.astype(bf16)


def centroid_kernel(rel_ref, slab_ref, rhs1_ref, lhs2_ref, wk_ref, out_ref, acc_ref):
    item = pl.program_id(0)
    items = pl.num_programs(0)
    layers, slab_rows, width = slab_ref.shape
    rows = slab_rows - SPREAD - 8
    ph = jnp.zeros((rows, PUP), f32)
    for which_layer in range(layers):
        row_at = rel_ref[item * layers + which_layer]
        col_at = rel_ref[(items + item) * layers + which_layer]
        base = pl.multiple_of((row_at // 8) * 8, 8)
        window = slab_ref[which_layer, pl.ds(base, rows + 8), :]
        window = pltpu.roll(window, (rows + 8 - (row_at - base)) % (rows + 8), 0)
        window = pltpu.roll(window, (width - col_at) % width, 1)
        ph = ph + window[:rows, :PUP]
    fc = jnp.cos(ph).astype(bf16)
    fs = jnp.sin(ph).astype(bf16)
    rhs1 = rhs1_ref[...]
    lhs2 = lhs2_ref[...]
    wk = wk_ref[...]
    rows = ph.shape[0]
    sub_rows = rows // SAMP
    groups = ph.shape[1] // LANES
    half = rhs1.shape[1] // 2
    lhs = jnp.concatenate(
        [
            jnp.concatenate([fc[:, g * LANES:(g + 1) * LANES], fs[:, g * LANES:(g + 1) * LANES]] * 2, axis=1)
            for g in range(groups)
        ],
        axis=0,
    )
    t_all = jnp.dot(lhs, rhs1, preferred_element_type=f32)
    weights = (lax.broadcasted_iota(jnp.int32, (sub_rows, NPIX, 2 * half), 1) - NPIX // 2).astype(f32)
    for g in range(groups):
        t = t_all[g * rows:(g + 1) * rows]
        tc = jnp.concatenate([t[:, :half], t[:, half:]], axis=0)
        t_hi = tc.astype(bf16)
        t_lo = (tc - t_hi.astype(f32)).astype(bf16)
        s = jnp.dot(lhs2, jnp.concatenate([t_hi, t_lo, t_hi], axis=0), preferred_element_type=f32)
        sr = s[:rows * 2]
        si = s[rows * 2:]
        inten = (sr * sr + si * si).reshape(sub_rows, NPIX, half)
        acc_ref[g, 0:sub_rows, :] = jnp.sum(inten, axis=1)
        acc_ref[g, sub_rows:2 * sub_rows, :] = jnp.sum(inten * weights[:, :, :half], axis=1)
        acc_ref[g, 2 * sub_rows:, :] = jnp.zeros((acc_ref.shape[1] - 2 * sub_rows, half), f32)
    pj = acc_ref[...].reshape(groups * acc_ref.shape[1], half)
    p_hi = pj.astype(bf16)
    p_lo = (pj - p_hi.astype(f32)).astype(bf16)
    q = jnp.dot(p_hi, wk, preferred_element_type=f32) + jnp.dot(p_lo, wk, preferred_element_type=f32)
    out_ref[0] = q.reshape(groups, acc_ref.shape[1], wk.shape[1])


def centroids_kernel(slabs, rel, sub_rows, items):
    rows = sub_rows * SAMP
    groups = PUP // LANES
    width = -(-slabs.shape[2] // LANES) * LANES
    slabs = jnp.pad(slabs.astype(f32), ((0, 0), (0, 8), (0, width - slabs.shape[2])))
    rhs1, lhs2, wk = dft_operands(sub_rows)
    sums = pl.pallas_call(
        centroid_kernel,
        grid_spec=pltpu.PrefetchScalarGridSpec(
            num_scalar_prefetch=1,
            grid=(items,),
            in_specs=[
                pl.BlockSpec(slabs.shape, lambda i, r: (0, 0, 0)),
                pl.BlockSpec(rhs1.shape, lambda i, r: (0, 0)),
                pl.BlockSpec(lhs2.shape, lambda i, r: (0, 0)),
                pl.BlockSpec(wk.shape, lambda i, r: (0, 0)),
            ],
            out_specs=pl.BlockSpec((1, groups, 16, 16), lambda i, r: (i, 0, 0, 0)),
            scratch_shapes=[pltpu.VMEM((groups, 16, rhs1.shape[1] // 2), f32)],
        ),
        out_shape=jax.ShapeDtypeStruct((items, groups, 16, 16), f32),
    )(rel.reshape(-1), slabs, rhs1, lhs2, wk)
    lane_subs = LANES // SAMP
    sums = sums.transpose(0, 2, 1, 3)
    flux = sums[:, :sub_rows, :, :lane_subs].reshape(items, sub_rows, -1)
    sum_x = sums[:, :sub_rows, :, lane_subs:2 * lane_subs].reshape(items, sub_rows, -1)
    sum_y = sums[:, sub_rows:2 * sub_rows, :, :lane_subs].reshape(items, sub_rows, -1)
    return jnp.stack([sum_x / flux, sum_y / flux], axis=-1)


def body(screens, offsets, valid, recon):
    narrow_count = lax.axis_size("narrow")
    wide_index = lax.axis_index("wide")
    narrow_index = lax.axis_index("narrow")
    band_rows = screens.shape[1]
    sub_rows = valid.shape[1]
    pixel_rows = sub_rows * SAMP
    slab_rows = pixel_rows + SPREAD
    union_cols = PUP + SPREAD
    local_items = FR_DEV * NSENS
    own_offsets = lax.dynamic_slice_in_dim(offsets, wide_index * local_items, local_items, 1)
    lowest = jnp.min(offsets, axis=1)
    pad = jnp.zeros((slab_rows, union_cols), screens.dtype)
    slabs = []
    for which_layer in range(L):
        band = lax.dynamic_slice(
            screens, (which_layer, 0, lowest[1, which_layer]), (1, band_rows, union_cols)
        )[0]
        padded = jnp.concatenate([pad, band, pad], axis=0)
        group_start = lowest[0, which_layer] + pixel_rows * narrow_index
        row_at = jnp.clip(group_start - wide_index * band_rows + slab_rows, 0, band_rows + slab_rows)
        slabs.append(lax.dynamic_slice_in_dim(padded, row_at, slab_rows, 0))
    slabs = lax.psum(jnp.stack(slabs), "wide")
    rel = own_offsets - lowest[:, None, :]
    measured = centroids_kernel(slabs, rel, sub_rows, local_items)
    measured = measured.reshape(FR_DEV, NSENS, sub_rows, NSUB, 2) * valid[None, :, :, :, None].astype(
        jnp.float32
    )
    slopes = measured.transpose(4, 0, 1, 2, 3)
    slope_vector = (
        measured.transpose(0, 2, 1, 3, 4)
        .reshape(FR_DEV, sub_rows * NSENS * NSUB * 2)
        .astype(jnp.bfloat16)
    )
    partial_commands = jnp.dot(
        lax.all_gather(slope_vector, "wide", axis=0, tiled=True),
        recon,
        preferred_element_type=jnp.float32,
    )
    partial_commands = partial_commands.reshape(narrow_count, -1, partial_commands.shape[1])
    commands = jnp.sum(lax.all_to_all(partial_commands, "narrow", 0, 0), axis=0)
    return (slopes, commands)


def solution(mesh):
    return jax.shard_map(
        body,
        mesh=mesh,
        in_specs=(P(None, "wide", None), P(), P(None, "narrow", None), P("narrow", "wide")),
        out_specs=(P(None, "wide", None, "narrow", None), P("narrow", "wide")),
        check_vma=False,
    )
```

```python
import math

import jax
import jax.numpy as jnp
from jax import lax
from jax.experimental import pallas as pl
from jax.experimental.pallas import tpu as pltpu
from jax.sharding import PartitionSpec as P

L = 4
NSUB = 80
SAMP = 16
NPIX = 32
NSENS = 2
SPREAD = 64
FR_DEV = 4
PUP = 1280
LANES = 128
f32 = jnp.float32
bf16 = jnp.bfloat16


def split_hi_lo(x):
    hi = lax.reduce_precision(x, exponent_bits=8, mantissa_bits=7)
    return hi.astype(bf16), (x - hi).astype(bf16)


def dft_factors(samp, npix):
    ids = jnp.arange(samp, dtype=jnp.int32)
    pix = jnp.arange(npix, dtype=jnp.int32) - npix // 2
    turns = jnp.mod(pix[:, None] * ids[None, :], npix)
    angles = turns.astype(f32) * f32(-2.0 * math.pi / npix)
    return jnp.cos(angles), jnp.sin(angles)


def block_diag(block, count):
    eye = jnp.eye(count, dtype=block.dtype)
    p, q = block.shape
    return (eye[:, None, :, None] * block[None, :, None, :]).reshape(count * p, count * q)


def dft_operands(sub_rows):
    lane_subs = LANES // SAMP
    cosf, sinf = dft_factors(SAMP, NPIX)
    bc = block_diag(cosf.T, lane_subs)
    bs = block_diag(sinf.T, lane_subs)
    rhs1 = jnp.concatenate([jnp.concatenate([bc, bs], 1), jnp.concatenate([-bs, bc], 1)], 0)
    r1_hi, r1_lo = split_hi_lo(rhs1)
    rhs1 = jnp.concatenate([r1_hi, r1_lo], 0)
    ac = block_diag(cosf, sub_rows)
    as_ = block_diag(sinf, sub_rows)
    m2 = jnp.concatenate([jnp.concatenate([ac, -as_], 1), jnp.concatenate([as_, ac], 1)], 0)
    m_hi, m_lo = split_hi_lo(m2)
    lhs2 = jnp.concatenate([m_hi, m_hi, m_lo], axis=1)
    weights = jnp.arange(NPIX, dtype=f32) - NPIX // 2
    ones = jnp.ones((NPIX,), f32)
    eye_c = jnp.eye(lane_subs, dtype=f32)
    wk = jnp.concatenate([(eye_c[:, None, :] * ones[None, :, None]).reshape(-1, lane_subs),
                          (eye_c[:, None, :] * weights[None, :, None]).reshape(-1, lane_subs)], 1)
    return rhs1, lhs2, wk.astype(bf16)


def centroid_kernel(rel_ref, slab_ref, rhs1_ref, lhs2_ref, wk_ref, out_ref, acc_ref):
    item = pl.program_id(0)
    items = pl.num_programs(0)
    layers, slab_rows, width = slab_ref.shape
    rows = slab_rows - SPREAD - 16
    span = PUP + SPREAD + LANES - SPREAD
    ph = jnp.zeros((rows, PUP), f32)
    for which_layer in range(layers):
        row_at = rel_ref[item * layers + which_layer]
        col_at = rel_ref[(items + item) * layers + which_layer]
        base = pl.multiple_of((row_at // 16) * 16, 16)
        col_base = pl.multiple_of((col_at // LANES) * LANES, LANES)
        window = slab_ref[which_layer, pl.ds(base, rows + 16), pl.ds(col_base, span)].astype(f32)
        window = pltpu.roll(window, (rows + 16 - (row_at - base)) % (rows + 16), 0)
        window = pltpu.roll(window, (span - (col_at - col_base)) % span, 1)
        ph = ph + window[:rows, :PUP]
    fc = jnp.cos(ph).astype(bf16)
    fs = jnp.sin(ph).astype(bf16)
    rhs1 = rhs1_ref[...]
    lhs2 = lhs2_ref[...]
    wk = wk_ref[...]
    rows = ph.shape[0]
    sub_rows = rows // SAMP
    groups = ph.shape[1] // LANES
    half = rhs1.shape[1] // 2
    lhs = jnp.concatenate(
        [
            jnp.concatenate([fc[:, g * LANES:(g + 1) * LANES], fs[:, g * LANES:(g + 1) * LANES]] * 2, axis=1)
            for g in range(groups)
        ],
        axis=0,
    )
    t_all = jnp.dot(lhs, rhs1, preferred_element_type=f32)
    weights = (lax.broadcasted_iota(jnp.int32, (sub_rows, NPIX, 2 * half), 1) - NPIX // 2).astype(f32)
    for g in range(groups):
        t = t_all[g * rows:(g + 1) * rows]
        tc = jnp.concatenate([t[:, :half], t[:, half:]], axis=0)
        t_hi = tc.astype(bf16)
        t_lo = (tc - t_hi.astype(f32)).astype(bf16)
        s = jnp.dot(lhs2, jnp.concatenate([t_hi, t_lo, t_hi], axis=0), preferred_element_type=f32)
        sr = s[:rows * 2]
        si = s[rows * 2:]
        inten = (sr * sr + si * si).reshape(sub_rows, NPIX, half)
        acc_ref[g, 0:sub_rows, :] = jnp.sum(inten, axis=1)
        acc_ref[g, sub_rows:2 * sub_rows, :] = jnp.sum(inten * weights[:, :, :half], axis=1)
        acc_ref[g, 2 * sub_rows:, :] = jnp.zeros((acc_ref.shape[1] - 2 * sub_rows, half), f32)
    pj = acc_ref[...].reshape(groups * acc_ref.shape[1], half)
    p_hi = pj.astype(bf16)
    p_lo = (pj - p_hi.astype(f32)).astype(bf16)
    q = jnp.dot(p_hi, wk, preferred_element_type=f32) + jnp.dot(p_lo, wk, preferred_element_type=f32)
    out_ref[0] = q.reshape(groups, acc_ref.shape[1], wk.shape[1])


def centroids_kernel(slabs, rel, sub_rows, items):
    rows = sub_rows * SAMP
    groups = PUP // LANES
    rhs1, lhs2, wk = dft_operands(sub_rows)
    sums = pl.pallas_call(
        centroid_kernel,
        grid_spec=pltpu.PrefetchScalarGridSpec(
            num_scalar_prefetch=1,
            grid=(items,),
            in_specs=[
                pl.BlockSpec(slabs.shape, lambda i, r: (0, 0, 0)),
                pl.BlockSpec(rhs1.shape, lambda i, r: (0, 0)),
                pl.BlockSpec(lhs2.shape, lambda i, r: (0, 0)),
                pl.BlockSpec(wk.shape, lambda i, r: (0, 0)),
            ],
            out_specs=pl.BlockSpec((1, groups, 16, 16), lambda i, r: (i, 0, 0, 0)),
            scratch_shapes=[pltpu.VMEM((groups, 16, rhs1.shape[1] // 2), f32)],
        ),
        out_shape=jax.ShapeDtypeStruct((items, groups, 16, 16), f32),
    )(rel.reshape(-1), slabs, rhs1, lhs2, wk)
    lane_subs = LANES // SAMP
    sums = sums.transpose(0, 2, 1, 3)
    flux = sums[:, :sub_rows, :, :lane_subs].reshape(items, sub_rows, -1)
    sum_x = sums[:, :sub_rows, :, lane_subs:2 * lane_subs].reshape(items, sub_rows, -1)
    sum_y = sums[:, sub_rows:2 * sub_rows, :, :lane_subs].reshape(items, sub_rows, -1)
    return jnp.stack([sum_x / flux, sum_y / flux], axis=-1)


def body(screens, offsets, valid, recon):
    narrow_count = lax.axis_size("narrow")
    wide_index = lax.axis_index("wide")
    narrow_index = lax.axis_index("narrow")
    band_rows = screens.shape[1]
    sub_rows = valid.shape[1]
    pixel_rows = sub_rows * SAMP
    slab_rows = pixel_rows + SPREAD
    union_cols = PUP + SPREAD
    local_items = FR_DEV * NSENS
    own_offsets = lax.dynamic_slice_in_dim(offsets, wide_index * local_items, local_items, 1)
    lowest = jnp.min(offsets, axis=1)
    picked = slab_rows + 16
    local_row = jnp.arange(band_rows, dtype=jnp.int32)
    slabs = []
    for which_layer in range(L):
        first = lowest[0, which_layer] + pixel_rows * narrow_index - wide_index * band_rows
        wanted = first + jnp.arange(picked, dtype=jnp.int32)
        select = (wanted[:, None] == local_row[None, :]).astype(screens.dtype)
        rows_of = jnp.dot(select, screens[which_layer], preferred_element_type=f32)
        slabs.append(rows_of.astype(screens.dtype))
    slabs = lax.psum(jnp.stack(slabs), "wide")
    rel = jnp.stack([own_offsets[0] - lowest[0][None, :], own_offsets[1]])
    measured = centroids_kernel(slabs, rel, sub_rows, local_items)
    measured = measured.reshape(FR_DEV, NSENS, sub_rows, NSUB, 2) * valid[None, :, :, :, None].astype(
        jnp.float32
    )
    slopes = measured.transpose(4, 0, 1, 2, 3)
    slope_vector = (
        measured.transpose(0, 2, 1, 3, 4)
        .reshape(FR_DEV, sub_rows * NSENS * NSUB * 2)
        .astype(jnp.bfloat16)
    )
    partial_commands = jnp.dot(
        lax.all_gather(slope_vector, "wide", axis=0, tiled=True),
        recon,
        preferred_element_type=jnp.float32,
    )
    partial_commands = partial_commands.reshape(narrow_count, -1, partial_commands.shape[1])
    commands = jnp.sum(lax.all_to_all(partial_commands, "narrow", 0, 0), axis=0)
    return (slopes, commands)


def solution(mesh):
    return jax.shard_map(
        body,
        mesh=mesh,
        in_specs=(P(None, "wide", None), P(), P(None, "narrow", None), P("narrow", "wide")),
        out_specs=(P(None, "wide", None, "narrow", None), P("narrow", "wide")),
        check_vma=False,
    )
```

```python
import math

import jax
import jax.numpy as jnp
from jax import lax
from jax.experimental import pallas as pl
from jax.experimental.pallas import tpu as pltpu
from jax.sharding import PartitionSpec as P

L = 4
NSUB = 80
SAMP = 16
NPIX = 32
NSENS = 2
SPREAD = 64
FR_DEV = 4
PUP = 1280
LANES = 128
f32 = jnp.float32
bf16 = jnp.bfloat16


def split_hi_lo(x):
    hi = lax.reduce_precision(x, exponent_bits=8, mantissa_bits=7)
    return hi.astype(bf16), (x - hi).astype(bf16)


def dft_factors(samp, npix):
    ids = jnp.arange(samp, dtype=jnp.int32)
    pix = jnp.arange(npix, dtype=jnp.int32) - npix // 2
    turns = jnp.mod(pix[:, None] * ids[None, :], npix)
    angles = turns.astype(f32) * f32(-2.0 * math.pi / npix)
    return jnp.cos(angles), jnp.sin(angles)


def block_diag(block, count):
    eye = jnp.eye(count, dtype=block.dtype)
    p, q = block.shape
    return (eye[:, None, :, None] * block[None, :, None, :]).reshape(count * p, count * q)


def dft_operands(sub_rows):
    lane_subs = LANES // SAMP
    cosf, sinf = dft_factors(SAMP, NPIX)
    bc = block_diag(cosf.T, lane_subs)
    bs = block_diag(sinf.T, lane_subs)
    rhs1 = jnp.concatenate([jnp.concatenate([bc, bs], 1), jnp.concatenate([-bs, bc], 1)], 0)
    r1_hi, r1_lo = split_hi_lo(rhs1)
    rhs1 = jnp.concatenate([r1_hi, r1_lo], 0)
    ac = block_diag(cosf, sub_rows)
    as_ = block_diag(sinf, sub_rows)
    m2 = jnp.concatenate([jnp.concatenate([ac, -as_], 1), jnp.concatenate([as_, ac], 1)], 0)
    m_hi, m_lo = split_hi_lo(m2)
    lhs2 = jnp.concatenate([m_hi, m_hi, m_lo], axis=1)
    weights = jnp.arange(NPIX, dtype=f32) - NPIX // 2
    ones = jnp.ones((NPIX,), f32)
    eye_c = jnp.eye(lane_subs, dtype=f32)
    wk = jnp.concatenate([(eye_c[:, None, :] * ones[None, :, None]).reshape(-1, lane_subs),
                          (eye_c[:, None, :] * weights[None, :, None]).reshape(-1, lane_subs)], 1)
    return rhs1, lhs2, wk.astype(bf16)


def centroid_kernel(rel_ref, slab_ref, rhs1_ref, lhs2_ref, wk_ref, out_ref, acc_ref):
    item = pl.program_id(0)
    items = pl.num_programs(0)
    layers, slab_rows, width = slab_ref.shape
    rows = slab_rows - SPREAD - 16
    ph = jnp.zeros((rows, PUP), f32)
    for which_layer in range(layers):
        row_at = rel_ref[item * layers + which_layer]
        col_at = rel_ref[(items + item) * layers + which_layer]
        base = pl.multiple_of((row_at // 16) * 16, 16)
        window = slab_ref[which_layer, pl.ds(base, rows + 16), :].astype(f32)
        window = pltpu.roll(window, (rows + 16 - (row_at - base)) % (rows + 16), 0)
        window = pltpu.roll(window, (width - col_at) % width, 1)
        ph = ph + window[:rows, :PUP]
    fc = jnp.cos(ph).astype(bf16)
    fs = jnp.sin(ph).astype(bf16)
    rhs1 = rhs1_ref[...]
    lhs2 = lhs2_ref[...]
    wk = wk_ref[...]
    rows = ph.shape[0]
    sub_rows = rows // SAMP
    groups = ph.shape[1] // LANES
    half = rhs1.shape[1] // 2
    lhs = jnp.concatenate(
        [
            jnp.concatenate([fc[:, g * LANES:(g + 1) * LANES], fs[:, g * LANES:(g + 1) * LANES]] * 2, axis=1)
            for g in range(groups)
        ],
        axis=0,
    )
    t_all = jnp.dot(lhs, rhs1, preferred_element_type=f32)
    weights = (lax.broadcasted_iota(jnp.int32, (sub_rows, NPIX, 2 * half), 1) - NPIX // 2).astype(f32)
    for g in range(groups):
        t = t_all[g * rows:(g + 1) * rows]
        tc = jnp.concatenate([t[:, :half], t[:, half:]], axis=0)
        t_hi = tc.astype(bf16)
        t_lo = (tc - t_hi.astype(f32)).astype(bf16)
        s = jnp.dot(lhs2, jnp.concatenate([t_hi, t_lo, t_hi], axis=0), preferred_element_type=f32)
        sr = s[:rows * 2]
        si = s[rows * 2:]
        inten = (sr * sr + si * si).reshape(sub_rows, NPIX, half)
        acc_ref[g, 0:sub_rows, :] = jnp.sum(inten, axis=1)
        acc_ref[g, sub_rows:2 * sub_rows, :] = jnp.sum(inten * weights[:, :, :half], axis=1)
        acc_ref[g, 2 * sub_rows:, :] = jnp.zeros((acc_ref.shape[1] - 2 * sub_rows, half), f32)
    pj = acc_ref[...].reshape(groups * acc_ref.shape[1], half)
    p_hi = pj.astype(bf16)
    p_lo = (pj - p_hi.astype(f32)).astype(bf16)
    q = jnp.dot(p_hi, wk, preferred_element_type=f32) + jnp.dot(p_lo, wk, preferred_element_type=f32)
    out_ref[0] = q.reshape(groups, acc_ref.shape[1], wk.shape[1])


def centroids_kernel(slabs, rel, sub_rows, items):
    rows = sub_rows * SAMP
    groups = PUP // LANES
    rhs1, lhs2, wk = dft_operands(sub_rows)
    sums = pl.pallas_call(
        centroid_kernel,
        grid_spec=pltpu.PrefetchScalarGridSpec(
            num_scalar_prefetch=1,
            grid=(items,),
            in_specs=[
                pl.BlockSpec(slabs.shape, lambda i, r: (0, 0, 0)),
                pl.BlockSpec(rhs1.shape, lambda i, r: (0, 0)),
                pl.BlockSpec(lhs2.shape, lambda i, r: (0, 0)),
                pl.BlockSpec(wk.shape, lambda i, r: (0, 0)),
            ],
            out_specs=pl.BlockSpec((1, groups, 16, 16), lambda i, r: (i, 0, 0, 0)),
            scratch_shapes=[pltpu.VMEM((groups, 16, rhs1.shape[1] // 2), f32)],
        ),
        out_shape=jax.ShapeDtypeStruct((items, groups, 16, 16), f32),
    )(rel.reshape(-1), slabs, rhs1, lhs2, wk)
    lane_subs = LANES // SAMP
    sums = sums.transpose(0, 2, 1, 3)
    flux = sums[:, :sub_rows, :, :lane_subs].reshape(items, sub_rows, -1)
    sum_x = sums[:, :sub_rows, :, lane_subs:2 * lane_subs].reshape(items, sub_rows, -1)
    sum_y = sums[:, sub_rows:2 * sub_rows, :, :lane_subs].reshape(items, sub_rows, -1)
    return jnp.stack([sum_x / flux, sum_y / flux], axis=-1)


def body(screens, offsets, valid, recon):
    narrow_count = lax.axis_size("narrow")
    wide_index = lax.axis_index("wide")
    narrow_index = lax.axis_index("narrow")
    band_rows = screens.shape[1]
    sub_rows = valid.shape[1]
    pixel_rows = sub_rows * SAMP
    slab_rows = pixel_rows + SPREAD + 16
    union_cols = PUP + LANES
    local_items = FR_DEV * NSENS
    own_offsets = lax.dynamic_slice_in_dim(offsets, wide_index * local_items, local_items, 1)
    lowest = jnp.min(offsets, axis=1)
    pad = jnp.zeros((slab_rows, union_cols), screens.dtype)
    slabs = []
    for which_layer in range(L):
        band = lax.dynamic_slice(
            screens, (which_layer, 0, lowest[1, which_layer]), (1, band_rows, union_cols)
        )[0]
        padded = jnp.concatenate([pad, band, pad], axis=0)
        group_start = lowest[0, which_layer] + pixel_rows * narrow_index
        row_at = jnp.clip(group_start - wide_index * band_rows + slab_rows, 0, band_rows + slab_rows)
        slabs.append(lax.dynamic_slice_in_dim(padded, row_at, slab_rows, 0))
    slabs = lax.psum(jnp.stack(slabs), "wide")
    rel = own_offsets - lowest[:, None, :]
    measured = centroids_kernel(slabs, rel, sub_rows, local_items)
    measured = measured.reshape(FR_DEV, NSENS, sub_rows, NSUB, 2) * valid[None, :, :, :, None].astype(
        jnp.float32
    )
    slopes = measured.transpose(4, 0, 1, 2, 3)
    slope_vector = (
        measured.transpose(0, 2, 1, 3, 4)
        .reshape(FR_DEV, sub_rows * NSENS * NSUB * 2)
        .astype(jnp.bfloat16)
    )
    partial_commands = jnp.dot(
        lax.all_gather(slope_vector, "wide", axis=0, tiled=True),
        recon,
        preferred_element_type=jnp.float32,
    )
    partial_commands = partial_commands.reshape(narrow_count, -1, partial_commands.shape[1])
    commands = jnp.sum(lax.all_to_all(partial_commands, "narrow", 0, 0), axis=0)
    return (slopes, commands)


def solution(mesh):
    return jax.shard_map(
        body,
        mesh=mesh,
        in_specs=(P(None, "wide", None), P(), P(None, "narrow", None), P("narrow", "wide")),
        out_specs=(P(None, "wide", None, "narrow", None), P("narrow", "wide")),
        check_vma=False,
    )
```

```python
import math

import jax
import jax.numpy as jnp
from jax import lax
from jax.experimental import pallas as pl
from jax.experimental.pallas import tpu as pltpu
from jax.sharding import PartitionSpec as P

L = 4
NSUB = 80
SAMP = 16
NPIX = 32
NSENS = 2
SPREAD = 64
FR_DEV = 4
PUP = 1280
LANES = 128
f32 = jnp.float32
bf16 = jnp.bfloat16


def split_hi_lo(x):
    hi = lax.reduce_precision(x, exponent_bits=8, mantissa_bits=7)
    return hi.astype(bf16), (x - hi).astype(bf16)


def dft_factors(samp, npix):
    ids = jnp.arange(samp, dtype=jnp.int32)
    pix = jnp.arange(npix, dtype=jnp.int32) - npix // 2
    turns = jnp.mod(pix[:, None] * ids[None, :], npix)
    angles = turns.astype(f32) * f32(-2.0 * math.pi / npix)
    return jnp.cos(angles), jnp.sin(angles)


def block_diag(block, count):
    eye = jnp.eye(count, dtype=block.dtype)
    p, q = block.shape
    return (eye[:, None, :, None] * block[None, :, None, :]).reshape(count * p, count * q)


def dft_operands(sub_rows):
    lane_subs = LANES // SAMP
    cosf, sinf = dft_factors(SAMP, NPIX)
    bc = block_diag(cosf.T, lane_subs)
    bs = block_diag(sinf.T, lane_subs)
    rhs1 = jnp.concatenate([jnp.concatenate([bc, bs], 1), jnp.concatenate([-bs, bc], 1)], 0)
    r1_hi, r1_lo = split_hi_lo(rhs1)
    rhs1 = jnp.concatenate([r1_hi, r1_lo], 0)
    ac = block_diag(cosf, sub_rows)
    as_ = block_diag(sinf, sub_rows)
    m2 = jnp.concatenate([jnp.concatenate([ac, -as_], 1), jnp.concatenate([as_, ac], 1)], 0)
    m_hi, m_lo = split_hi_lo(m2)
    lhs2 = jnp.concatenate([m_hi, m_hi, m_lo], axis=1)
    weights = jnp.arange(NPIX, dtype=f32) - NPIX // 2
    ones = jnp.ones((NPIX,), f32)
    eye_c = jnp.eye(lane_subs, dtype=f32)
    wk = jnp.concatenate([(eye_c[:, None, :] * ones[None, :, None]).reshape(-1, lane_subs),
                          (eye_c[:, None, :] * weights[None, :, None]).reshape(-1, lane_subs)], 1)
    return rhs1, lhs2, wk.astype(bf16)


def centroid_kernel(rel_ref, slab_ref, rhs1_ref, lhs2_ref, wk_ref, out_ref, acc_ref):
    item = pl.program_id(0)
    items = pl.num_programs(0)
    layers, slab_rows, width = slab_ref.shape
    rows = slab_rows - SPREAD - 16
    ph = jnp.zeros((rows, PUP), f32)
    for which_layer in range(layers):
        row_at = rel_ref[item * layers + which_layer]
        col_at = rel_ref[(items + item) * layers + which_layer]
        base = pl.multiple_of((row_at // 16) * 16, 16)
        window = slab_ref[which_layer, pl.ds(base, rows + 16), :].astype(f32)
        window = pltpu.roll(window, (rows + 16 - (row_at - base)) % (rows + 16), 0)
        window = pltpu.roll(window, (width - col_at) % width, 1)
        ph = ph + window[:rows, :PUP]
    fc = jnp.cos(ph).astype(bf16)
    fs = jnp.sin(ph).astype(bf16)
    rhs1 = rhs1_ref[...]
    lhs2 = lhs2_ref[...]
    wk = wk_ref[...]
    rows = ph.shape[0]
    sub_rows = rows // SAMP
    groups = ph.shape[1] // LANES
    half = rhs1.shape[1] // 2
    lhs = jnp.concatenate(
        [
            jnp.concatenate([fc[:, g * LANES:(g + 1) * LANES], fs[:, g * LANES:(g + 1) * LANES]] * 2, axis=1)
            for g in range(groups)
        ],
        axis=0,
    )
    t_all = jnp.dot(lhs, rhs1, preferred_element_type=f32)
    weights = (lax.broadcasted_iota(jnp.int32, (sub_rows, NPIX, 2 * half), 1) - NPIX // 2).astype(f32)
    for g in range(groups):
        t = t_all[g * rows:(g + 1) * rows]
        tc = jnp.concatenate([t[:, :half], t[:, half:]], axis=0)
        t_hi = tc.astype(bf16)
        t_lo = (tc - t_hi.astype(f32)).astype(bf16)
        s = jnp.dot(lhs2, jnp.concatenate([t_hi, t_lo, t_hi], axis=0), preferred_element_type=f32)
        sr = s[:rows * 2]
        si = s[rows * 2:]
        inten = (sr * sr + si * si).reshape(sub_rows, NPIX, half)
        acc_ref[g, 0:sub_rows, :] = jnp.sum(inten, axis=1)
        acc_ref[g, sub_rows:2 * sub_rows, :] = jnp.sum(inten * weights[:, :, :half], axis=1)
        acc_ref[g, 2 * sub_rows:, :] = jnp.zeros((acc_ref.shape[1] - 2 * sub_rows, half), f32)
    pj = acc_ref[...].reshape(groups * acc_ref.shape[1], half)
    p_hi = pj.astype(bf16)
    p_lo = (pj - p_hi.astype(f32)).astype(bf16)
    q = jnp.dot(p_hi, wk, preferred_element_type=f32) + jnp.dot(p_lo, wk, preferred_element_type=f32)
    out_ref[0] = q.reshape(groups, acc_ref.shape[1], wk.shape[1])


def centroids_kernel(slabs, rel, sub_rows, items):
    rows = sub_rows * SAMP
    groups = PUP // LANES
    rhs1, lhs2, wk = dft_operands(sub_rows)
    sums = pl.pallas_call(
        centroid_kernel,
        grid_spec=pltpu.PrefetchScalarGridSpec(
            num_scalar_prefetch=1,
            grid=(items,),
            in_specs=[
                pl.BlockSpec(slabs.shape, lambda i, r: (0, 0, 0)),
                pl.BlockSpec(rhs1.shape, lambda i, r: (0, 0)),
                pl.BlockSpec(lhs2.shape, lambda i, r: (0, 0)),
                pl.BlockSpec(wk.shape, lambda i, r: (0, 0)),
            ],
            out_specs=pl.BlockSpec((1, groups, 16, 16), lambda i, r: (i, 0, 0, 0)),
            scratch_shapes=[pltpu.VMEM((groups, 16, rhs1.shape[1] // 2), f32)],
        ),
        out_shape=jax.ShapeDtypeStruct((items, groups, 16, 16), f32),
    )(rel.reshape(-1), slabs, rhs1, lhs2, wk)
    lane_subs = LANES // SAMP
    sums = sums.transpose(0, 2, 1, 3)
    flux = sums[:, :sub_rows, :, :lane_subs].reshape(items, sub_rows, -1)
    sum_x = sums[:, :sub_rows, :, lane_subs:2 * lane_subs].reshape(items, sub_rows, -1)
    sum_y = sums[:, sub_rows:2 * sub_rows, :, :lane_subs].reshape(items, sub_rows, -1)
    return jnp.stack([sum_x / flux, sum_y / flux], axis=-1)


def body(screens, offsets, valid, recon):
    narrow_count = lax.axis_size("narrow")
    wide_index = lax.axis_index("wide")
    narrow_index = lax.axis_index("narrow")
    band_rows = screens.shape[1]
    sub_rows = valid.shape[1]
    pixel_rows = sub_rows * SAMP
    slab_rows = pixel_rows + SPREAD + 16
    union_cols = PUP + LANES
    local_items = FR_DEV * NSENS
    own_offsets = lax.dynamic_slice_in_dim(offsets, wide_index * local_items, local_items, 1)
    lowest = jnp.min(offsets, axis=1)
    local_row = jnp.arange(band_rows, dtype=jnp.int32)
    slabs = []
    for which_layer in range(L):
        band = lax.dynamic_slice(
            screens, (which_layer, 0, lowest[1, which_layer]), (1, band_rows, union_cols)
        )[0]
        first = lowest[0, which_layer] + pixel_rows * narrow_index - wide_index * band_rows
        wanted = first + jnp.arange(slab_rows, dtype=jnp.int32)
        select = (wanted[:, None] == local_row[None, :]).astype(screens.dtype)
        slabs.append(jnp.dot(select, band, preferred_element_type=f32).astype(screens.dtype))
    slabs = lax.psum(jnp.stack(slabs), "wide")
    rel = own_offsets - lowest[:, None, :]
    measured = centroids_kernel(slabs, rel, sub_rows, local_items)
    measured = measured.reshape(FR_DEV, NSENS, sub_rows, NSUB, 2) * valid[None, :, :, :, None].astype(
        jnp.float32
    )
    slopes = measured.transpose(4, 0, 1, 2, 3)
    slope_vector = (
        measured.transpose(0, 2, 1, 3, 4)
        .reshape(FR_DEV, sub_rows * NSENS * NSUB * 2)
        .astype(jnp.bfloat16)
    )
    partial_commands = jnp.dot(
        lax.all_gather(slope_vector, "wide", axis=0, tiled=True),
        recon,
        preferred_element_type=jnp.float32,
    )
    partial_commands = partial_commands.reshape(narrow_count, -1, partial_commands.shape[1])
    commands = jnp.sum(lax.all_to_all(partial_commands, "narrow", 0, 0), axis=0)
    return (slopes, commands)


def solution(mesh):
    return jax.shard_map(
        body,
        mesh=mesh,
        in_specs=(P(None, "wide", None), P(), P(None, "narrow", None), P("narrow", "wide")),
        out_specs=(P(None, "wide", None, "narrow", None), P("narrow", "wide")),
        check_vma=False,
    )
```
